512 devices in a mesh: tgt: 16 (over z), src: 32 (over x, y, core).
Axes of the slice: x: 4, y: 4, z: 16, core: 2. Of those that a mesh axis runs over, the one named last changes fastest.
Arguments:
- target_xy: float32 [2, 8192], P(None, 'tgt'), may hold values from 0 to 20
- source_xy: float32 [2, 65536], P(None, 'src'), may hold values from 0 to 20
- body_of: int32 [65536], P('src'), may hold values from 0 to 127
- series_coef: float32 [2, 32, 128], replicated, may hold values from -2 to 2
- probe_matrix: bfloat16 [65536, 128], P('src'), may hold values from -0.0234375 to 0.0234375
- row_weight: float32 [8192], P('tgt'), may hold values from 1 to 36
Outputs:
- basis: float32 [8192, 256], P(('tgt', 'src'))
- factor: float32 [128, 128], replicated
The draws below stay inside these ranges and needn't reach their ends.
All inputs are finite; a program needn't handle non-finite values.
Results may differ from the reference program's by a relative error of at most 0.0085.
Values sent between devices are 32-bit elements; how exact they have to be, the bound alone decides.
No kernel may reach another device: no remote copies, remote signals or barrier semaphores. Data moves between devices by JAX's collectives and lax.ppermute only.
A program may use at most 64 MiB of HBM per device.

```python
import jax
import jax.numpy as jnp
from jax import lax

T_DEV = 512
S_DEV = 2048
K = 128
NTERMS = 32
BODIES = 128
TARGETS = 8192
SOURCES = 65536
N_TGT = 16
N_SRC = 32


def draw_row_weight(key, part):
    spread = jax.random.uniform(key, (TARGETS,), jnp.float32)
    place = jnp.arange(TARGETS).astype(jnp.float32) / TARGETS
    return jnp.exp(jnp.log(4.0) * spread) * jnp.exp(jnp.log(3.0) * place)


def place_ends(array, rng, low, top_value):
    spot = [jax.random.randint(jax.random.fold_in(rng, axis), (), 0, length) for axis, length in enumerate(array.shape)]
    main_axis = array.shape.index(max(array.shape))
    beside = spot[:main_axis] + [(spot[main_axis] + 1) % array.shape[main_axis]] + spot[main_axis + 1:]
    return array.at[tuple(spot)].set(low).at[tuple(beside)].set(top_value)


def levels(key, extent, cuts, low, top_value):
    def one(axis_at, shards_of):
        steps = jax.random.uniform(jax.random.fold_in(jax.random.fold_in(key, 6), axis_at), (shards_of,), jnp.float32, low / len(cuts), top_value / len(cuts))
        return jnp.repeat(jnp.exp(steps), extent[axis_at] // shards_of).reshape((-1,) + (1,) * (len(extent) - axis_at - 1))

    gain = one(*cuts[0])
    for cut in cuts[1:]:
        gain = gain * one(*cut)
    return gain


def bell_draw(stream_key, shape, width, bound, shards=(), kind=jnp.bfloat16):
    entries = width * jax.random.normal(stream_key, shape, jnp.float32)
    if shards:
        entries = entries * levels(stream_key, shape, shards, -0.22, 0.18)
    return jnp.clip(entries, -bound, bound).astype(kind)


def setup_inputs(seed: int = 0) -> dict:
    streams_of = jax.random.split(jax.random.key(seed), 7)
    target_xy = jnp.clip(20.0 * jax.random.uniform(streams_of[0], (2, TARGETS), jnp.float32) ** levels(streams_of[0], (2, TARGETS), ((1, 16),), -0.2, 0.2), 0.0, 20.0)
    source_xy = jnp.clip(20.0 * jax.random.uniform(streams_of[1], (2, SOURCES), jnp.float32) ** levels(streams_of[1], (2, SOURCES), ((1, 32),), -0.2, 0.2), 0.0, 20.0)
    body_of = place_ends(jax.random.randint(streams_of[2], (SOURCES,), 0, BODIES), jax.random.fold_in(streams_of[2], 1), 0, BODIES - 1).astype(jnp.int32)
    series_coef = bell_draw(streams_of[3], (2, NTERMS, BODIES), 0.3, 2.0, (), jnp.float32)
    probe_matrix = bell_draw(streams_of[4], (SOURCES, K), SOURCES ** -0.5, 0.0234375, ((0, 32),))
    row_weight = draw_row_weight(jax.random.fold_in(streams_of[6], 71), 0)
    return dict(target_xy=target_xy, source_xy=source_xy, body_of=body_of, series_coef=series_coef, probe_matrix=probe_matrix, row_weight=row_weight)


def panel_series(rows_xy, cols_xy, coef_re, coef_im):
    delta_x = rows_xy[0][:, None] - cols_xy[0][None, :]
    delta_y = rows_xy[1][:, None] - cols_xy[1][None, :]
    radius = jnp.sqrt(delta_x * delta_x + delta_y * delta_y + 0.25)
    decay_rate = jnp.exp(-0.005 * radius)
    step_re = decay_rate * jnp.cos(1.5 * radius)
    step_im = decay_rate * jnp.sin(1.5 * radius)
    term_count = coef_re.shape[0]
    total_re = jnp.broadcast_to(coef_re[term_count - 1][None, :], radius.shape)
    total_im = jnp.broadcast_to(coef_im[term_count - 1][None, :], radius.shape)
    for degree in range(term_count - 2, -1, -1):
        next_re = total_re * step_re - total_im * step_im + coef_re[degree][None, :]
        next_im = total_re * step_im + total_im * step_re + coef_im[degree][None, :]
        total_re, total_im = (next_re, next_im)
    series_re = total_re * step_re - total_im * step_im
    series_im = total_re * step_im + total_im * step_re
    tile_re = (1.0 / radius + series_re).astype(jnp.bfloat16)
    tile_im = series_im.astype(jnp.bfloat16)
    return (tile_re, tile_im)

def reference(target_xy, source_xy, body_of, series_coef, probe_matrix, row_weight):
    picked = series_coef[:, :, body_of]
    src_xy = source_xy.reshape(2, N_SRC, S_DEV).transpose(1, 0, 2)
    src_coef = picked.reshape(2, NTERMS, N_SRC, S_DEV).transpose(2, 0, 1, 3)
    src_probe = probe_matrix.reshape(N_SRC, S_DEV, K)

    def one_rows(rows_xy):

        def add_block(totals, pieces):
            xy_block, coef_block, probe_block = pieces
            tile_re, tile_im = panel_series(rows_xy, xy_block, coef_block[0], coef_block[1])
            part_re = jnp.dot(tile_re.astype(jnp.float32), probe_block.astype(jnp.float32), preferred_element_type=jnp.float32)
            part_im = jnp.dot(tile_im.astype(jnp.float32), probe_block.astype(jnp.float32), preferred_element_type=jnp.float32)
            return (totals + jnp.concatenate([part_re, part_im], axis=1), None)
        start_totals = jnp.zeros((rows_xy.shape[1], 2 * K), jnp.float32)
        totals, _ = lax.scan(add_block, start_totals, (src_xy, src_coef, src_probe))
        return totals
    tgt_blocks = target_xy.reshape(2, N_TGT, T_DEV).transpose(1, 0, 2)
    sketch = lax.map(one_rows, tgt_blocks).reshape(TARGETS, 2 * K)
    weighted = sketch * row_weight[:, None]
    stacked = weighted.reshape(2 * TARGETS, K)
    gram = jnp.dot(stacked.T, stacked, precision=lax.Precision.HIGHEST) / (2.0 * TARGETS)
    lower_factor = jnp.linalg.cholesky(gram)
    identity = jnp.eye(K, dtype=jnp.float32)
    inverse = lax.linalg.triangular_solve(lower_factor, identity, left_side=True, lower=True)
    basis = jnp.dot(stacked, inverse.T, precision=lax.Precision.HIGHEST).reshape(TARGETS, 2 * K)
    return (basis, lower_factor.T)
```

```python
import math

import jax
import jax.numpy as jnp
from jax import lax
from jax.sharding import PartitionSpec as P

NTERMS = 32


def in_blocks(array, dim, count):
    shape = array.shape
    tiles = array.reshape(*shape[:dim], count, shape[dim] // count, *shape[dim + 1 :])
    return jnp.moveaxis(tiles, dim, 0)


def sent_and_summed(array, axis, dim):
    tiles = in_blocks(array, dim, lax.axis_size(axis))
    arrived = lax.all_to_all(tiles, axis, split_axis=0, concat_axis=0, tiled=True)
    return arrived.sum(axis=0)


def from_everyone(array, axis):
    copies = jnp.broadcast_to(array, (lax.axis_size(axis), *array.shape))
    return lax.all_to_all(copies, axis, split_axis=0, concat_axis=0, tiled=True)


def of_everyone(array, axis):
    everything = from_everyone(array, axis)
    return jnp.sum(everything, axis=0)


def panel_series(rows_xy, cols_xy, coef_re, coef_im):
    delta_x = rows_xy[0][:, None] - cols_xy[0][None, :]
    delta_y = rows_xy[1][:, None] - cols_xy[1][None, :]
    radius = jnp.sqrt(delta_x * delta_x + delta_y * delta_y + 0.25)
    decay_rate = jnp.exp(-0.005 * radius)
    step_re = decay_rate * jnp.cos(1.5 * radius)
    step_im = decay_rate * jnp.sin(1.5 * radius)
    term_count = coef_re.shape[0]
    total_re = jnp.broadcast_to(coef_re[term_count - 1][None, :], radius.shape)
    total_im = jnp.broadcast_to(coef_im[term_count - 1][None, :], radius.shape)
    for degree in range(term_count - 2, -1, -1):
        next_re = total_re * step_re - total_im * step_im + coef_re[degree][None, :]
        next_im = total_re * step_im + total_im * step_re + coef_im[degree][None, :]
        total_re, total_im = (next_re, next_im)
    series_re = total_re * step_re - total_im * step_im
    series_im = total_re * step_im + total_im * step_re
    tile_re = (1.0 / radius + series_re).astype(jnp.bfloat16)
    tile_im = series_im.astype(jnp.bfloat16)
    return (tile_re, tile_im)


def sketch_rows(target_xy, source_xy, picked, probe_matrix, row_count):
    source_count = probe_matrix.shape[0]
    block_width = math.gcd(source_count, 1024)
    blocks = source_count // block_width
    rank_width = probe_matrix.shape[1]

    def add_block(block_index, totals):
        block_start = block_index * block_width
        xy_block = lax.dynamic_slice_in_dim(source_xy, block_start, block_width, 1)
        coef_block = lax.dynamic_slice_in_dim(picked, block_start, block_width, 1)
        probe_block = lax.dynamic_slice_in_dim(probe_matrix, block_start, block_width, 0)
        tile_re, tile_im = panel_series(
            target_xy, xy_block, coef_block[:NTERMS], coef_block[NTERMS:]
        )
        part_re = jnp.dot(tile_re, probe_block, preferred_element_type=jnp.float32)
        part_im = jnp.dot(tile_im, probe_block, preferred_element_type=jnp.float32)
        return totals + jnp.concatenate([part_re, part_im], axis=1)

    start_totals = jnp.zeros((row_count, 2 * rank_width), jnp.float32)
    return lax.fori_loop(0, blocks, add_block, start_totals)


def gram_of(rows_part, scale_rows):
    rank_width = rows_part.shape[1] // 2
    stacked = rows_part.reshape(-1, rank_width)
    return jnp.dot(stacked.T, stacked, precision=lax.Precision.HIGHEST) / scale_rows


def pick_coefficients(series_coef, body_of):
    bodies = series_coef.shape[2]
    one_hot = (jnp.arange(bodies, dtype=jnp.int32)[:, None] == body_of[None, :]).astype(
        jnp.bfloat16
    )
    table = series_coef.reshape(-1, bodies)
    high_part = table.astype(jnp.bfloat16)
    rest_one = table - high_part.astype(jnp.float32)
    middle_part = rest_one.astype(jnp.bfloat16)
    low_part = (rest_one - middle_part.astype(jnp.float32)).astype(jnp.bfloat16)
    picked = jnp.dot(high_part, one_hot, preferred_element_type=jnp.float32)
    picked = picked + jnp.dot(middle_part, one_hot, preferred_element_type=jnp.float32)
    return picked + jnp.dot(low_part, one_hot, preferred_element_type=jnp.float32)


def per_device(target_xy, source_xy, body_of, series_coef, probe_matrix, row_weight):
    rank_width = probe_matrix.shape[1]
    picked = pick_coefficients(series_coef, body_of)
    rows_all = target_xy.shape[1]
    own_count = rows_all // lax.axis_size("src")
    scale_rows = float(2 * rows_all * lax.axis_size("tgt"))
    own_start = lax.axis_index("src") * own_count
    own_sum = lax.psum_scatter(
        sketch_rows(target_xy, source_xy, picked, probe_matrix, own_count * lax.axis_size("src")),
        "src",
        scatter_dimension=0,
        tiled=True,
    )
    own_weight = lax.dynamic_slice_in_dim(row_weight, own_start, own_count, 0)
    own_rows = own_sum * own_weight[:, None]
    local_gram = gram_of(own_rows, scale_rows)
    full_gram = lax.psum(local_gram, ("tgt", "src"))
    lower_factor = jnp.linalg.cholesky(full_gram)
    identity = jnp.eye(rank_width, dtype=jnp.float32)
    inverse = lax.linalg.triangular_solve(lower_factor, identity, left_side=True, lower=True)
    basis_rows = jnp.dot(
        own_rows.reshape(-1, rank_width), inverse.T, precision=lax.Precision.HIGHEST
    )
    return (basis_rows.reshape(own_count, 2 * rank_width), lower_factor.T)


def solution(mesh):
    return jax.shard_map(
        per_device,
        mesh=mesh,
        in_specs=(P(None, "tgt"), P(None, "src"), P("src"), P(), P("src", None), P("tgt")),
        out_specs=(P(("tgt", "src"), None), P()),
        check_vma=False,
    )
```

```python
import math

import jax
import jax.numpy as jnp
from jax import lax
from jax.sharding import PartitionSpec as P

NTERMS = 32


def in_blocks(array, dim, count):
    shape = array.shape
    tiles = array.reshape(*shape[:dim], count, shape[dim] // count, *shape[dim + 1 :])
    return jnp.moveaxis(tiles, dim, 0)


def sent_and_summed(array, axis, dim):
    tiles = in_blocks(array, dim, lax.axis_size(axis))
    arrived = lax.all_to_all(tiles, axis, split_axis=0, concat_axis=0, tiled=True)
    return arrived.sum(axis=0)


def from_everyone(array, axis):
    copies = jnp.broadcast_to(array, (lax.axis_size(axis), *array.shape))
    return lax.all_to_all(copies, axis, split_axis=0, concat_axis=0, tiled=True)


def of_everyone(array, axis):
    everything = from_everyone(array, axis)
    return jnp.sum(everything, axis=0)


def panel_series(rows_xy, cols_xy, coef_re, coef_im):
    delta_x = rows_xy[0][:, None] - cols_xy[0][None, :]
    delta_y = rows_xy[1][:, None] - cols_xy[1][None, :]
    radius = jnp.sqrt(delta_x * delta_x + delta_y * delta_y + 0.25)
    decay_rate = jnp.exp(-0.005 * radius)
    step_re = decay_rate * jnp.cos(1.5 * radius)
    step_im = decay_rate * jnp.sin(1.5 * radius)
    term_count = coef_re.shape[0]
    total_re = jnp.broadcast_to(coef_re[term_count - 1][None, :], radius.shape)
    total_im = jnp.broadcast_to(coef_im[term_count - 1][None, :], radius.shape)
    for degree in range(term_count - 2, -1, -1):
        next_re = total_re * step_re - total_im * step_im + coef_re[degree][None, :]
        next_im = total_re * step_im + total_im * step_re + coef_im[degree][None, :]
        total_re, total_im = (next_re, next_im)
    series_re = total_re * step_re - total_im * step_im
    series_im = total_re * step_im + total_im * step_re
    tile_re = (1.0 / radius + series_re).astype(jnp.bfloat16)
    tile_im = series_im.astype(jnp.bfloat16)
    return (tile_re, tile_im)


def sketch_rows(target_xy, source_xy, picked, probe_matrix, row_count):
    source_count = probe_matrix.shape[0]
    block_width = math.gcd(source_count, 1024)
    blocks = source_count // block_width
    rank_width = probe_matrix.shape[1]

    def add_block(block_index, totals):
        block_start = block_index * block_width
        xy_block = lax.dynamic_slice_in_dim(source_xy, block_start, block_width, 1)
        coef_block = lax.dynamic_slice_in_dim(picked, block_start, block_width, 1)
        probe_block = lax.dynamic_slice_in_dim(probe_matrix, block_start, block_width, 0)
        tile_re, tile_im = panel_series(
            target_xy, xy_block, coef_block[:NTERMS], coef_block[NTERMS:]
        )
        part_re = jnp.dot(tile_re, probe_block, preferred_element_type=jnp.float32)
        part_im = jnp.dot(tile_im, probe_block, preferred_element_type=jnp.float32)
        return totals + jnp.concatenate([part_re, part_im], axis=1)

    start_totals = jnp.zeros((row_count, 2 * rank_width), jnp.float32)
    return lax.fori_loop(0, blocks, add_block, start_totals)


def gram_of(rows_part, scale_rows):
    rank_width = rows_part.shape[1] // 2
    stacked = rows_part.reshape(-1, rank_width)
    return jnp.dot(stacked.T, stacked, precision=lax.Precision.HIGHEST) / scale_rows


def pick_coefficients(series_coef, body_of):
    bodies = series_coef.shape[2]
    one_hot = (jnp.arange(bodies, dtype=jnp.int32)[:, None] == body_of[None, :]).astype(
        jnp.bfloat16
    )
    table = series_coef.reshape(-1, bodies)
    high_part = table.astype(jnp.bfloat16)
    rest_one = table - high_part.astype(jnp.float32)
    middle_part = rest_one.astype(jnp.bfloat16)
    low_part = (rest_one - middle_part.astype(jnp.float32)).astype(jnp.bfloat16)
    picked = jnp.dot(high_part, one_hot, preferred_element_type=jnp.float32)
    picked = picked + jnp.dot(middle_part, one_hot, preferred_element_type=jnp.float32)
    return picked + jnp.dot(low_part, one_hot, preferred_element_type=jnp.float32)


def per_device(target_xy, source_xy, body_of, series_coef, probe_matrix, row_weight):
    rank_width = probe_matrix.shape[1]
    picked = pick_coefficients(series_coef, body_of)
    rows_all = target_xy.shape[1]
    own_count = rows_all // lax.axis_size("src")
    scale_rows = float(2 * rows_all * lax.axis_size("tgt"))
    own_start = lax.axis_index("src") * own_count
    own_sum = sent_and_summed(
        sketch_rows(target_xy, source_xy, picked, probe_matrix, own_count * lax.axis_size("src")),
        "src",
        0,
    )
    own_weight = lax.dynamic_slice_in_dim(row_weight, own_start, own_count, 0)
    own_rows = own_sum * own_weight[:, None]
    local_gram = gram_of(own_rows, scale_rows)
    gram_piece = sent_and_summed(local_gram, "src", 0)
    gram_piece = of_everyone(gram_piece, "tgt")
    full_gram = from_everyone(gram_piece, "src").reshape(rank_width, rank_width)
    lower_factor = jnp.linalg.cholesky(full_gram)
    identity = jnp.eye(rank_width, dtype=jnp.float32)
    inverse = lax.linalg.triangular_solve(lower_factor, identity, left_side=True, lower=True)
    basis_rows = jnp.dot(
        own_rows.reshape(-1, rank_width), inverse.T, precision=lax.Precision.HIGHEST
    )
    return (basis_rows.reshape(own_count, 2 * rank_width), lower_factor.T)


def solution(mesh):
    return jax.shard_map(
        per_device,
        mesh=mesh,
        in_specs=(P(None, "tgt"), P(None, "src"), P("src"), P(), P("src", None), P("tgt")),
        out_specs=(P(("tgt", "src"), None), P()),
        check_vma=False,
    )
```

```python
import math

import jax
import jax.numpy as jnp
from jax import lax
from jax.experimental import pallas as pl
from jax.experimental.pallas import tpu as pltpu
from jax.sharding import PartitionSpec as P

NTERMS = 32
SUB_ROWS = 32
LANES = 128
COL_BLOCK = 512


def sketch_kernel(txy_ref, sxy_ref, coef_ref, probe_ref, out_ref, re_scr, im_scr):
    col_step = pl.program_id(0)
    rows = re_scr.shape[0]
    groups = re_scr.shape[1] // LANES
    terms = coef_ref.shape[0] // 2

    @pl.when(col_step == 0)
    def _():
        out_ref[...] = jnp.zeros_like(out_ref)

    def one_sub(index, carry):
        row_at = pl.multiple_of((index // groups) * SUB_ROWS, SUB_ROWS)
        col_at = pl.multiple_of((index % groups) * LANES, LANES)
        tx = txy_ref[0, pl.ds(row_at, SUB_ROWS), :]
        ty = txy_ref[1, pl.ds(row_at, SUB_ROWS), :]
        sx = sxy_ref[pl.ds(0, 1), pl.ds(col_at, LANES)]
        sy = sxy_ref[pl.ds(1, 1), pl.ds(col_at, LANES)]
        delta_x = tx - sx
        delta_y = ty - sy
        radius = jnp.sqrt(delta_x * delta_x + delta_y * delta_y + 0.25)
        decay_rate = jnp.exp(-0.005 * radius)
        step_re = decay_rate * jnp.cos(1.5 * radius)
        step_im = decay_rate * jnp.sin(1.5 * radius)

        def coef(n):
            return (coef_ref[pl.ds(n, 1), pl.ds(col_at, LANES)],
                    coef_ref[pl.ds(terms + n, 1), pl.ds(col_at, LANES)])

        last_re, last_im = coef(terms - 1)
        total_re = jnp.broadcast_to(last_re, radius.shape)
        total_im = jnp.broadcast_to(last_im, radius.shape)
        for degree in range(terms - 2, -1, -1):
            c_re, c_im = coef(degree)
            next_re = total_re * step_re - total_im * step_im + c_re
            next_im = total_re * step_im + total_im * step_re + c_im
            total_re, total_im = next_re, next_im
        series_re = total_re * step_re - total_im * step_im
        series_im = total_re * step_im + total_im * step_re
        re_scr[pl.ds(row_at, SUB_ROWS), pl.ds(col_at, LANES)] = (1.0 / radius + series_re).astype(jnp.bfloat16)
        im_scr[pl.ds(row_at, SUB_ROWS), pl.ds(col_at, LANES)] = series_im.astype(jnp.bfloat16)
        return carry

    lax.fori_loop(0, (rows // SUB_ROWS) * groups, one_sub, 0)
    probe = probe_ref[...]
    rank = probe.shape[1]
    out_ref[:, :rank] += jnp.dot(re_scr[...], probe, preferred_element_type=jnp.float32)
    out_ref[:, rank:] += jnp.dot(im_scr[...], probe, preferred_element_type=jnp.float32)


def sketch_pallas(target_xy, source_xy, picked, probe_matrix):
    rows = target_xy.shape[1]
    sources = source_xy.shape[1]
    rank = probe_matrix.shape[1]
    col_block = min(COL_BLOCK, sources)
    txy = jnp.broadcast_to(target_xy[:, :, None], (2, rows, LANES))
    return pl.pallas_call(
        sketch_kernel,
        grid=(sources // col_block,),
        in_specs=[
            pl.BlockSpec((2, rows, LANES), lambda j: (0, 0, 0)),
            pl.BlockSpec((2, col_block), lambda j: (0, j)),
            pl.BlockSpec((picked.shape[0], col_block), lambda j: (0, j)),
            pl.BlockSpec((col_block, rank), lambda j: (j, 0)),
        ],
        out_specs=pl.BlockSpec((rows, 2 * rank), lambda j: (0, 0)),
        out_shape=jax.ShapeDtypeStruct((rows, 2 * rank), jnp.float32),
        scratch_shapes=[pltpu.VMEM((rows, col_block), jnp.bfloat16),
                        pltpu.VMEM((rows, col_block), jnp.bfloat16)],
    )(txy, source_xy, picked, probe_matrix)


def in_blocks(array, dim, count):
    shape = array.shape
    tiles = array.reshape(*shape[:dim], count, shape[dim] // count, *shape[dim + 1 :])
    return jnp.moveaxis(tiles, dim, 0)


def sent_and_summed(array, axis, dim):
    tiles = in_blocks(array, dim, lax.axis_size(axis))
    arrived = lax.all_to_all(tiles, axis, split_axis=0, concat_axis=0, tiled=True)
    return arrived.sum(axis=0)


def from_everyone(array, axis):
    copies = jnp.broadcast_to(array, (lax.axis_size(axis), *array.shape))
    return lax.all_to_all(copies, axis, split_axis=0, concat_axis=0, tiled=True)


def of_everyone(array, axis):
    everything = from_everyone(array, axis)
    return jnp.sum(everything, axis=0)


def panel_series(rows_xy, cols_xy, coef_re, coef_im):
    delta_x = rows_xy[0][:, None] - cols_xy[0][None, :]
    delta_y = rows_xy[1][:, None] - cols_xy[1][None, :]
    radius = jnp.sqrt(delta_x * delta_x + delta_y * delta_y + 0.25)
    decay_rate = jnp.exp(-0.005 * radius)
    step_re = decay_rate * jnp.cos(1.5 * radius)
    step_im = decay_rate * jnp.sin(1.5 * radius)
    term_count = coef_re.shape[0]
    total_re = jnp.broadcast_to(coef_re[term_count - 1][None, :], radius.shape)
    total_im = jnp.broadcast_to(coef_im[term_count - 1][None, :], radius.shape)
    for degree in range(term_count - 2, -1, -1):
        next_re = total_re * step_re - total_im * step_im + coef_re[degree][None, :]
        next_im = total_re * step_im + total_im * step_re + coef_im[degree][None, :]
        total_re, total_im = (next_re, next_im)
    series_re = total_re * step_re - total_im * step_im
    series_im = total_re * step_im + total_im * step_re
    tile_re = (1.0 / radius + series_re).astype(jnp.bfloat16)
    tile_im = series_im.astype(jnp.bfloat16)
    return (tile_re, tile_im)


def sketch_rows(target_xy, source_xy, picked, probe_matrix, row_count):
    source_count = probe_matrix.shape[0]
    block_width = math.gcd(source_count, 1024)
    blocks = source_count // block_width
    rank_width = probe_matrix.shape[1]

    def add_block(block_index, totals):
        block_start = block_index * block_width
        xy_block = lax.dynamic_slice_in_dim(source_xy, block_start, block_width, 1)
        coef_block = lax.dynamic_slice_in_dim(picked, block_start, block_width, 1)
        probe_block = lax.dynamic_slice_in_dim(probe_matrix, block_start, block_width, 0)
        tile_re, tile_im = panel_series(
            target_xy, xy_block, coef_block[:NTERMS], coef_block[NTERMS:]
        )
        part_re = jnp.dot(tile_re, probe_block, preferred_element_type=jnp.float32)
        part_im = jnp.dot(tile_im, probe_block, preferred_element_type=jnp.float32)
        return totals + jnp.concatenate([part_re, part_im], axis=1)

    start_totals = jnp.zeros((row_count, 2 * rank_width), jnp.float32)
    return lax.fori_loop(0, blocks, add_block, start_totals)


def gram_of(rows_part, scale_rows):
    rank_width = rows_part.shape[1] // 2
    stacked = rows_part.reshape(-1, rank_width)
    return jnp.dot(stacked.T, stacked, precision=lax.Precision.HIGHEST) / scale_rows


def pick_coefficients(series_coef, body_of):
    bodies = series_coef.shape[2]
    one_hot = (jnp.arange(bodies, dtype=jnp.int32)[:, None] == body_of[None, :]).astype(
        jnp.bfloat16
    )
    table = series_coef.reshape(-1, bodies)
    high_part = table.astype(jnp.bfloat16)
    rest_one = table - high_part.astype(jnp.float32)
    middle_part = rest_one.astype(jnp.bfloat16)
    low_part = (rest_one - middle_part.astype(jnp.float32)).astype(jnp.bfloat16)
    picked = jnp.dot(high_part, one_hot, preferred_element_type=jnp.float32)
    picked = picked + jnp.dot(middle_part, one_hot, preferred_element_type=jnp.float32)
    return picked + jnp.dot(low_part, one_hot, preferred_element_type=jnp.float32)


def per_device(target_xy, source_xy, body_of, series_coef, probe_matrix, row_weight):
    rank_width = probe_matrix.shape[1]
    picked = pick_coefficients(series_coef, body_of)
    rows_all = target_xy.shape[1]
    own_count = rows_all // lax.axis_size("src")
    scale_rows = float(2 * rows_all * lax.axis_size("tgt"))
    own_start = lax.axis_index("src") * own_count
    own_sum = sent_and_summed(
        sketch_pallas(target_xy, source_xy, picked, probe_matrix),
        "src",
        0,
    )
    own_weight = lax.dynamic_slice_in_dim(row_weight, own_start, own_count, 0)
    own_rows = own_sum * own_weight[:, None]
    local_gram = gram_of(own_rows, scale_rows)
    gram_piece = sent_and_summed(local_gram, "src", 0)
    gram_piece = of_everyone(gram_piece, "tgt")
    full_gram = from_everyone(gram_piece, "src").reshape(rank_width, rank_width)
    lower_factor = jnp.linalg.cholesky(full_gram)
    identity = jnp.eye(rank_width, dtype=jnp.float32)
    inverse = lax.linalg.triangular_solve(lower_factor, identity, left_side=True, lower=True)
    basis_rows = jnp.dot(
        own_rows.reshape(-1, rank_width), inverse.T, precision=lax.Precision.HIGHEST
    )
    return (basis_rows.reshape(own_count, 2 * rank_width), lower_factor.T)


def solution(mesh):
    return jax.shard_map(
        per_device,
        mesh=mesh,
        in_specs=(P(None, "tgt"), P(None, "src"), P("src"), P(), P("src", None), P("tgt")),
        out_specs=(P(("tgt", "src"), None), P()),
        check_vma=False,
    )
```

```python
import math

import jax
import jax.numpy as jnp
from jax import lax
from jax.experimental import pallas as pl
from jax.experimental.pallas import tpu as pltpu
from jax.sharding import PartitionSpec as P

NTERMS = 32
SUB_ROWS = 64
LANES = 128
COL_BLOCK = 512


def cos_and_sin(angle):
    quarter = jnp.floor(angle * 0.6366197723675814 + 0.5)
    rest = angle - quarter * 1.5703125
    rest = rest - quarter * 4.837512969970703125e-4
    rest = rest - quarter * 7.54978995489188216e-8
    square = rest * rest
    sin_rest = rest + rest * square * (
        -1.6666654611e-1 + square * (8.3321608736e-3 + square * -1.9515295891e-4)
    )
    cos_rest = (1.0 - 0.5 * square) + square * square * (
        4.166664568298827e-2 + square * (-1.388731625493765e-3 + square * 2.443315711809948e-5)
    )
    turn = quarter.astype(jnp.int32)
    swap = (turn & 1) == 1
    sin_value = jnp.where(swap, cos_rest, sin_rest)
    cos_value = jnp.where(swap, sin_rest, cos_rest)
    sin_value = jnp.where((turn & 2) == 2, -sin_value, sin_value)
    cos_value = jnp.where(((turn + 1) & 2) == 2, -cos_value, cos_value)
    return cos_value, sin_value


def sketch_kernel(txy_ref, sxy_ref, coef_ref, probe_ref, out_ref, re_scr, im_scr):
    col_step = pl.program_id(0)
    rows = re_scr.shape[0]
    groups = re_scr.shape[1] // LANES
    terms = coef_ref.shape[0] // 2

    @pl.when(col_step == 0)
    def _():
        out_ref[...] = jnp.zeros_like(out_ref)

    def one_sub(index, carry):
        row_at = pl.multiple_of((index // groups) * SUB_ROWS, SUB_ROWS)
        col_at = pl.multiple_of((index % groups) * LANES, LANES)
        tx = txy_ref[0, pl.ds(row_at, SUB_ROWS), :]
        ty = txy_ref[1, pl.ds(row_at, SUB_ROWS), :]
        sx = sxy_ref[pl.ds(0, 1), pl.ds(col_at, LANES)]
        sy = sxy_ref[pl.ds(1, 1), pl.ds(col_at, LANES)]
        delta_x = tx - sx
        delta_y = ty - sy
        radius = jnp.sqrt(delta_x * delta_x + delta_y * delta_y + 0.25)
        decay_rate = jnp.exp(-0.005 * radius)
        cos_part, sin_part = cos_and_sin(1.5 * radius)
        step_re = decay_rate * cos_part
        step_im = decay_rate * sin_part

        def coef(n):
            return (coef_ref[pl.ds(n, 1), pl.ds(col_at, LANES)],
                    coef_ref[pl.ds(terms + n, 1), pl.ds(col_at, LANES)])

        last_re, last_im = coef(terms - 1)
        total_re = jnp.broadcast_to(last_re, radius.shape)
        total_im = jnp.broadcast_to(last_im, radius.shape)
        for degree in range(terms - 2, -1, -1):
            c_re, c_im = coef(degree)
            next_re = total_re * step_re - total_im * step_im + c_re
            next_im = total_re * step_im + total_im * step_re + c_im
            total_re, total_im = next_re, next_im
        series_re = total_re * step_re - total_im * step_im
        series_im = total_re * step_im + total_im * step_re
        re_scr[pl.ds(row_at, SUB_ROWS), pl.ds(col_at, LANES)] = (1.0 / radius + series_re).astype(jnp.bfloat16)
        im_scr[pl.ds(row_at, SUB_ROWS), pl.ds(col_at, LANES)] = series_im.astype(jnp.bfloat16)
        return carry

    lax.fori_loop(0, (rows // SUB_ROWS) * groups, one_sub, 0, unroll=2)
    probe = probe_ref[...]
    rank = probe.shape[1]
    out_ref[:, :rank] += jnp.dot(re_scr[...], probe, preferred_element_type=jnp.float32)
    out_ref[:, rank:] += jnp.dot(im_scr[...], probe, preferred_element_type=jnp.float32)


def sketch_pallas(target_xy, source_xy, picked, probe_matrix):
    rows = target_xy.shape[1]
    sources = source_xy.shape[1]
    rank = probe_matrix.shape[1]
    col_block = min(COL_BLOCK, sources)
    txy = jnp.broadcast_to(target_xy[:, :, None], (2, rows, LANES))
    return pl.pallas_call(
        sketch_kernel,
        grid=(sources // col_block,),
        in_specs=[
            pl.BlockSpec((2, rows, LANES), lambda j: (0, 0, 0)),
            pl.BlockSpec((2, col_block), lambda j: (0, j)),
            pl.BlockSpec((picked.shape[0], col_block), lambda j: (0, j)),
            pl.BlockSpec((col_block, rank), lambda j: (j, 0)),
        ],
        out_specs=pl.BlockSpec((rows, 2 * rank), lambda j: (0, 0)),
        out_shape=jax.ShapeDtypeStruct((rows, 2 * rank), jnp.float32),
        scratch_shapes=[pltpu.VMEM((rows, col_block), jnp.bfloat16),
                        pltpu.VMEM((rows, col_block), jnp.bfloat16)],
    )(txy, source_xy, picked, probe_matrix)


def in_blocks(array, dim, count):
    shape = array.shape
    tiles = array.reshape(*shape[:dim], count, shape[dim] // count, *shape[dim + 1 :])
    return jnp.moveaxis(tiles, dim, 0)


def sent_and_summed(array, axis, dim):
    tiles = in_blocks(array, dim, lax.axis_size(axis))
    arrived = lax.all_to_all(tiles, axis, split_axis=0, concat_axis=0, tiled=True)
    return arrived.sum(axis=0)


def from_everyone(array, axis):
    copies = jnp.broadcast_to(array, (lax.axis_size(axis), *array.shape))
    return lax.all_to_all(copies, axis, split_axis=0, concat_axis=0, tiled=True)


def of_everyone(array, axis):
    everything = from_everyone(array, axis)
    return jnp.sum(everything, axis=0)


def panel_series(rows_xy, cols_xy, coef_re, coef_im):
    delta_x = rows_xy[0][:, None] - cols_xy[0][None, :]
    delta_y = rows_xy[1][:, None] - cols_xy[1][None, :]
    radius = jnp.sqrt(delta_x * delta_x + delta_y * delta_y + 0.25)
    decay_rate = jnp.exp(-0.005 * radius)
    step_re = decay_rate * jnp.cos(1.5 * radius)
    step_im = decay_rate * jnp.sin(1.5 * radius)
    term_count = coef_re.shape[0]
    total_re = jnp.broadcast_to(coef_re[term_count - 1][None, :], radius.shape)
    total_im = jnp.broadcast_to(coef_im[term_count - 1][None, :], radius.shape)
    for degree in range(term_count - 2, -1, -1):
        next_re = total_re * step_re - total_im * step_im + coef_re[degree][None, :]
        next_im = total_re * step_im + total_im * step_re + coef_im[degree][None, :]
        total_re, total_im = (next_re, next_im)
    series_re = total_re * step_re - total_im * step_im
    series_im = total_re * step_im + total_im * step_re
    tile_re = (1.0 / radius + series_re).astype(jnp.bfloat16)
    tile_im = series_im.astype(jnp.bfloat16)
    return (tile_re, tile_im)


def sketch_rows(target_xy, source_xy, picked, probe_matrix, row_count):
    source_count = probe_matrix.shape[0]
    block_width = math.gcd(source_count, 1024)
    blocks = source_count // block_width
    rank_width = probe_matrix.shape[1]

    def add_block(block_index, totals):
        block_start = block_index * block_width
        xy_block = lax.dynamic_slice_in_dim(source_xy, block_start, block_width, 1)
        coef_block = lax.dynamic_slice_in_dim(picked, block_start, block_width, 1)
        probe_block = lax.dynamic_slice_in_dim(probe_matrix, block_start, block_width, 0)
        tile_re, tile_im = panel_series(
            target_xy, xy_block, coef_block[:NTERMS], coef_block[NTERMS:]
        )
        part_re = jnp.dot(tile_re, probe_block, preferred_element_type=jnp.float32)
        part_im = jnp.dot(tile_im, probe_block, preferred_element_type=jnp.float32)
        return totals + jnp.concatenate([part_re, part_im], axis=1)

    start_totals = jnp.zeros((row_count, 2 * rank_width), jnp.float32)
    return lax.fori_loop(0, blocks, add_block, start_totals)


def gram_of(rows_part, scale_rows):
    rank_width = rows_part.shape[1] // 2
    stacked = rows_part.reshape(-1, rank_width)
    return jnp.dot(stacked.T, stacked, precision=lax.Precision.HIGHEST) / scale_rows


def pick_coefficients(series_coef, body_of):
    bodies = series_coef.shape[2]
    one_hot = (jnp.arange(bodies, dtype=jnp.int32)[:, None] == body_of[None, :]).astype(
        jnp.bfloat16
    )
    table = series_coef.reshape(-1, bodies)
    high_part = table.astype(jnp.bfloat16)
    rest_one = table - high_part.astype(jnp.float32)
    middle_part = rest_one.astype(jnp.bfloat16)
    low_part = (rest_one - middle_part.astype(jnp.float32)).astype(jnp.bfloat16)
    picked = jnp.dot(high_part, one_hot, preferred_element_type=jnp.float32)
    picked = picked + jnp.dot(middle_part, one_hot, preferred_element_type=jnp.float32)
    return picked + jnp.dot(low_part, one_hot, preferred_element_type=jnp.float32)


def per_device(target_xy, source_xy, body_of, series_coef, probe_matrix, row_weight):
    rank_width = probe_matrix.shape[1]
    picked = pick_coefficients(series_coef, body_of)
    rows_all = target_xy.shape[1]
    own_count = rows_all // lax.axis_size("src")
    scale_rows = float(2 * rows_all * lax.axis_size("tgt"))
    own_start = lax.axis_index("src") * own_count
    own_sum = sent_and_summed(
        sketch_pallas(target_xy, source_xy, picked, probe_matrix),
        "src",
        0,
    )
    own_weight = lax.dynamic_slice_in_dim(row_weight, own_start, own_count, 0)
    own_rows = own_sum * own_weight[:, None]
    local_gram = gram_of(own_rows, scale_rows)
    gram_piece = sent_and_summed(local_gram, "src", 0)
    gram_piece = of_everyone(gram_piece, "tgt")
    full_gram = from_everyone(gram_piece, "src").reshape(rank_width, rank_width)
    lower_factor = jnp.linalg.cholesky(full_gram)
    identity = jnp.eye(rank_width, dtype=jnp.float32)
    inverse = lax.linalg.triangular_solve(lower_factor, identity, left_side=True, lower=True)
    basis_rows = jnp.dot(
        own_rows.reshape(-1, rank_width), inverse.T, precision=lax.Precision.HIGHEST
    )
    return (basis_rows.reshape(own_count, 2 * rank_width), lower_factor.T)


def solution(mesh):
    return jax.shard_map(
        per_device,
        mesh=mesh,
        in_specs=(P(None, "tgt"), P(None, "src"), P("src"), P(), P("src", None), P("tgt")),
        out_specs=(P(("tgt", "src"), None), P()),
        check_vma=False,
    )
```

```python
import math

import jax
import jax.numpy as jnp
from jax import lax
from jax.experimental import pallas as pl
from jax.experimental.pallas import tpu as pltpu
from jax.sharding import PartitionSpec as P

NTERMS = 32
SUB_ROWS = 64
LANES = 128
COL_BLOCK = 512


def cos_and_sin(angle):
    quarter = jnp.floor(angle * 0.6366197723675814 + 0.5)
    rest = angle - quarter * 1.5703125
    rest = rest - quarter * 4.837512969970703125e-4
    rest = rest - quarter * 7.54978995489188216e-8
    square = rest * rest
    sin_rest = rest + rest * square * (
        -1.6666654611e-1 + square * (8.3321608736e-3 + square * -1.9515295891e-4)
    )
    cos_rest = (1.0 - 0.5 * square) + square * square * (
        4.166664568298827e-2 + square * (-1.388731625493765e-3 + square * 2.443315711809948e-5)
    )
    turn = quarter.astype(jnp.int32)
    swap = (turn & 1) == 1
    sin_value = jnp.where(swap, cos_rest, sin_rest)
    cos_value = jnp.where(swap, sin_rest, cos_rest)
    sin_value = jnp.where((turn & 2) == 2, -sin_value, sin_value)
    cos_value = jnp.where(((turn + 1) & 2) == 2, -cos_value, cos_value)
    return cos_value, sin_value


def sketch_kernel(txy_ref, sxy_ref, coef_ref, probe_ref, out_ref, re_scr, im_scr):
    col_step = pl.program_id(0)
    rows = re_scr.shape[0]
    groups = re_scr.shape[1] // LANES
    terms = coef_ref.shape[0] // 2

    @pl.when(col_step == 0)
    def _():
        out_ref[...] = jnp.zeros_like(out_ref)

    def one_sub(index, carry):
        row_at = pl.multiple_of((index // groups) * SUB_ROWS, SUB_ROWS)
        col_at = pl.multiple_of((index % groups) * LANES, LANES)
        tx = txy_ref[0, pl.ds(row_at, SUB_ROWS), :]
        ty = txy_ref[1, pl.ds(row_at, SUB_ROWS), :]
        sx = sxy_ref[pl.ds(0, 1), pl.ds(col_at, LANES)]
        sy = sxy_ref[pl.ds(1, 1), pl.ds(col_at, LANES)]
        delta_x = tx - sx
        delta_y = ty - sy
        radius = jnp.sqrt(delta_x * delta_x + delta_y * delta_y + 0.25)
        decay_rate = jnp.exp(-0.005 * radius)
        cos_part, sin_part = cos_and_sin(1.5 * radius)
        step_re = decay_rate * cos_part
        step_im = decay_rate * sin_part

        def coef(n):
            return (coef_ref[pl.ds(n, 1), pl.ds(col_at, LANES)],
                    coef_ref[pl.ds(terms + n, 1), pl.ds(col_at, LANES)])

        last_re, last_im = coef(terms - 1)
        total_re = jnp.broadcast_to(last_re, radius.shape)
        total_im = jnp.broadcast_to(last_im, radius.shape)
        for degree in range(terms - 2, -1, -1):
            c_re, c_im = coef(degree)
            next_re = total_re * step_re - total_im * step_im + c_re
            next_im = total_re * step_im + total_im * step_re + c_im
            total_re, total_im = next_re, next_im
        series_re = total_re * step_re - total_im * step_im
        series_im = total_re * step_im + total_im * step_re
        re_scr[pl.ds(row_at, SUB_ROWS), pl.ds(col_at, LANES)] = (1.0 / radius + series_re).astype(jnp.bfloat16)
        im_scr[pl.ds(row_at, SUB_ROWS), pl.ds(col_at, LANES)] = series_im.astype(jnp.bfloat16)
        return carry

    lax.fori_loop(0, (rows // SUB_ROWS) * groups, one_sub, 0, unroll=2)
    probe = probe_ref[...]
    rank = probe.shape[1]
    out_ref[:, :rank] += jnp.dot(re_scr[...], probe, preferred_element_type=jnp.float32)
    out_ref[:, rank:] += jnp.dot(im_scr[...], probe, preferred_element_type=jnp.float32)


def sketch_pallas(target_xy, source_xy, picked, probe_matrix):
    rows = target_xy.shape[1]
    sources = source_xy.shape[1]
    rank = probe_matrix.shape[1]
    col_block = min(COL_BLOCK, sources)
    txy = jnp.broadcast_to(target_xy[:, :, None], (2, rows, LANES))
    return pl.pallas_call(
        sketch_kernel,
        grid=(sources // col_block,),
        in_specs=[
            pl.BlockSpec((2, rows, LANES), lambda j: (0, 0, 0)),
            pl.BlockSpec((2, col_block), lambda j: (0, j)),
            pl.BlockSpec((picked.shape[0], col_block), lambda j: (0, j)),
            pl.BlockSpec((col_block, rank), lambda j: (j, 0)),
        ],
        out_specs=pl.BlockSpec((rows, 2 * rank), lambda j: (0, 0)),
        out_shape=jax.ShapeDtypeStruct((rows, 2 * rank), jnp.float32),
        scratch_shapes=[pltpu.VMEM((rows, col_block), jnp.bfloat16),
                        pltpu.VMEM((rows, col_block), jnp.bfloat16)],
    )(txy, source_xy, picked, probe_matrix)


def factor_kernel(gram_ref, upper_ref, inverse_ref):
    size = gram_ref.shape[0]
    upper_ref[...] = gram_ref[...]
    rows = lax.broadcasted_iota(jnp.int32, (size, size), 0)
    cols = lax.broadcasted_iota(jnp.int32, (size, size), 1)
    inverse_ref[...] = jnp.where(rows == cols, 1.0, 0.0).astype(jnp.float32)
    lane = lax.broadcasted_iota(jnp.int32, (1, size), 1)
    sublane = lax.broadcasted_iota(jnp.int32, (size, 1), 0)

    def step(j, carry):
        left = upper_ref[...]
        row_left = upper_ref[pl.ds(j, 1), :]
        row_right = inverse_ref[pl.ds(j, 1), :]
        pivot = jnp.sum(jnp.where(lane == j, row_left, 0.0), axis=1, keepdims=True)
        scale = 1.0 / jnp.sqrt(pivot)
        pivot_left = jnp.where(lane >= j, row_left * scale, 0.0)
        pivot_right = row_right * scale
        column = jnp.sum(jnp.where(cols == j, left, 0.0), axis=1, keepdims=True)
        multiplier = jnp.where(sublane > j, column * scale, 0.0)
        upper_ref[...] = left - multiplier * pivot_left
        inverse_ref[...] = inverse_ref[...] - multiplier * pivot_right
        upper_ref[pl.ds(j, 1), :] = pivot_left
        inverse_ref[pl.ds(j, 1), :] = pivot_right
        return carry

    lax.fori_loop(0, size, step, 0)
    upper_ref[...] = jnp.where(rows <= cols, upper_ref[...], 0.0)


def factor_pallas(gram):
    size = gram.shape[0]
    return pl.pallas_call(
        factor_kernel,
        out_shape=(jax.ShapeDtypeStruct((size, size), jnp.float32),
                   jax.ShapeDtypeStruct((size, size), jnp.float32)),
    )(gram)


def in_blocks(array, dim, count):
    shape = array.shape
    tiles = array.reshape(*shape[:dim], count, shape[dim] // count, *shape[dim + 1 :])
    return jnp.moveaxis(tiles, dim, 0)


def sent_and_summed(array, axis, dim):
    tiles = in_blocks(array, dim, lax.axis_size(axis))
    arrived = lax.all_to_all(tiles, axis, split_axis=0, concat_axis=0, tiled=True)
    return arrived.sum(axis=0)


def from_everyone(array, axis):
    copies = jnp.broadcast_to(array, (lax.axis_size(axis), *array.shape))
    return lax.all_to_all(copies, axis, split_axis=0, concat_axis=0, tiled=True)


def of_everyone(array, axis):
    everything = from_everyone(array, axis)
    return jnp.sum(everything, axis=0)


def panel_series(rows_xy, cols_xy, coef_re, coef_im):
    delta_x = rows_xy[0][:, None] - cols_xy[0][None, :]
    delta_y = rows_xy[1][:, None] - cols_xy[1][None, :]
    radius = jnp.sqrt(delta_x * delta_x + delta_y * delta_y + 0.25)
    decay_rate = jnp.exp(-0.005 * radius)
    step_re = decay_rate * jnp.cos(1.5 * radius)
    step_im = decay_rate * jnp.sin(1.5 * radius)
    term_count = coef_re.shape[0]
    total_re = jnp.broadcast_to(coef_re[term_count - 1][None, :], radius.shape)
    total_im = jnp.broadcast_to(coef_im[term_count - 1][None, :], radius.shape)
    for degree in range(term_count - 2, -1, -1):
        next_re = total_re * step_re - total_im * step_im + coef_re[degree][None, :]
        next_im = total_re * step_im + total_im * step_re + coef_im[degree][None, :]
        total_re, total_im = (next_re, next_im)
    series_re = total_re * step_re - total_im * step_im
    series_im = total_re * step_im + total_im * step_re
    tile_re = (1.0 / radius + series_re).astype(jnp.bfloat16)
    tile_im = series_im.astype(jnp.bfloat16)
    return (tile_re, tile_im)


def sketch_rows(target_xy, source_xy, picked, probe_matrix, row_count):
    source_count = probe_matrix.shape[0]
    block_width = math.gcd(source_count, 1024)
    blocks = source_count // block_width
    rank_width = probe_matrix.shape[1]

    def add_block(block_index, totals):
        block_start = block_index * block_width
        xy_block = lax.dynamic_slice_in_dim(source_xy, block_start, block_width, 1)
        coef_block = lax.dynamic_slice_in_dim(picked, block_start, block_width, 1)
        probe_block = lax.dynamic_slice_in_dim(probe_matrix, block_start, block_width, 0)
        tile_re, tile_im = panel_series(
            target_xy, xy_block, coef_block[:NTERMS], coef_block[NTERMS:]
        )
        part_re = jnp.dot(tile_re, probe_block, preferred_element_type=jnp.float32)
        part_im = jnp.dot(tile_im, probe_block, preferred_element_type=jnp.float32)
        return totals + jnp.concatenate([part_re, part_im], axis=1)

    start_totals = jnp.zeros((row_count, 2 * rank_width), jnp.float32)
    return lax.fori_loop(0, blocks, add_block, start_totals)


def gram_of(rows_part, scale_rows):
    rank_width = rows_part.shape[1] // 2
    stacked = rows_part.reshape(-1, rank_width)
    return jnp.dot(stacked.T, stacked, precision=lax.Precision.HIGHEST) / scale_rows


def pick_coefficients(series_coef, body_of):
    bodies = series_coef.shape[2]
    one_hot = (jnp.arange(bodies, dtype=jnp.int32)[:, None] == body_of[None, :]).astype(
        jnp.bfloat16
    )
    table = series_coef.reshape(-1, bodies)
    high_part = table.astype(jnp.bfloat16)
    rest_one = table - high_part.astype(jnp.float32)
    middle_part = rest_one.astype(jnp.bfloat16)
    low_part = (rest_one - middle_part.astype(jnp.float32)).astype(jnp.bfloat16)
    picked = jnp.dot(high_part, one_hot, preferred_element_type=jnp.float32)
    picked = picked + jnp.dot(middle_part, one_hot, preferred_element_type=jnp.float32)
    return picked + jnp.dot(low_part, one_hot, preferred_element_type=jnp.float32)


def per_device(target_xy, source_xy, body_of, series_coef, probe_matrix, row_weight):
    rank_width = probe_matrix.shape[1]
    picked = pick_coefficients(series_coef, body_of)
    rows_all = target_xy.shape[1]
    own_count = rows_all // lax.axis_size("src")
    scale_rows = float(2 * rows_all * lax.axis_size("tgt"))
    own_start = lax.axis_index("src") * own_count
    own_sum = sent_and_summed(
        sketch_pallas(target_xy, source_xy, picked, probe_matrix),
        "src",
        0,
    )
    own_weight = lax.dynamic_slice_in_dim(row_weight, own_start, own_count, 0)
    own_rows = own_sum * own_weight[:, None]
    local_gram = gram_of(own_rows, scale_rows)
    gram_piece = sent_and_summed(local_gram, "src", 0)
    gram_piece = of_everyone(gram_piece, "tgt")
    full_gram = from_everyone(gram_piece, "src").reshape(rank_width, rank_width)
    upper_factor, inverse = factor_pallas(full_gram)
    basis_rows = jnp.dot(
        own_rows.reshape(-1, rank_width), inverse.T, precision=lax.Precision.HIGHEST
    )
    return (basis_rows.reshape(own_count, 2 * rank_width), upper_factor)


def solution(mesh):
    return jax.shard_map(
        per_device,
        mesh=mesh,
        in_specs=(P(None, "tgt"), P(None, "src"), P("src"), P(), P("src", None), P("tgt")),
        out_specs=(P(("tgt", "src"), None), P()),
        check_vma=False,
    )
```

```python
import math

import jax
import jax.numpy as jnp
from jax import lax
from jax.experimental import pallas as pl
from jax.experimental.pallas import tpu as pltpu
from jax.sharding import PartitionSpec as P

NTERMS = 32
SUB_ROWS = 64
LANES = 128
COL_BLOCK = 512


def cos_and_sin(angle):
    quarter = jnp.floor(angle * 0.6366197723675814 + 0.5)
    rest = angle - quarter * 1.5703125
    rest = rest - quarter * 4.837512969970703125e-4
    rest = rest - quarter * 7.54978995489188216e-8
    square = rest * rest
    sin_rest = rest + rest * square * (
        -1.6666654611e-1 + square * (8.3321608736e-3 + square * -1.9515295891e-4)
    )
    cos_rest = (1.0 - 0.5 * square) + square * square * (
        4.166664568298827e-2 + square * (-1.388731625493765e-3 + square * 2.443315711809948e-5)
    )
    turn = quarter.astype(jnp.int32)
    swap = (turn & 1) == 1
    sin_value = jnp.where(swap, cos_rest, sin_rest)
    cos_value = jnp.where(swap, sin_rest, cos_rest)
    sin_value = jnp.where((turn & 2) == 2, -sin_value, sin_value)
    cos_value = jnp.where(((turn + 1) & 2) == 2, -cos_value, cos_value)
    return cos_value, sin_value


def sketch_kernel(txy_ref, sxy_ref, table_ref, body_ref, probe_ref, out_ref, coef_ref, re_scr, im_scr):
    col_step = pl.program_id(0)
    rows = re_scr.shape[0]
    groups = re_scr.shape[1] // LANES
    terms = coef_ref.shape[0] // 2

    @pl.when(col_step == 0)
    def _():
        out_ref[...] = jnp.zeros_like(out_ref)

    table = table_ref[...]
    bodies = table.shape[1]
    one_hot = (
        lax.broadcasted_iota(jnp.int32, (bodies, body_ref.shape[1]), 0) == body_ref[...]
    ).astype(jnp.bfloat16)
    high_part = table.astype(jnp.bfloat16)
    rest_one = table - high_part.astype(jnp.float32)
    middle_part = rest_one.astype(jnp.bfloat16)
    low_part = (rest_one - middle_part.astype(jnp.float32)).astype(jnp.bfloat16)
    picked = jnp.dot(high_part, one_hot, preferred_element_type=jnp.float32)
    picked = picked + jnp.dot(middle_part, one_hot, preferred_element_type=jnp.float32)
    coef_ref[...] = picked + jnp.dot(low_part, one_hot, preferred_element_type=jnp.float32)

    def one_sub(index, carry):
        row_at = pl.multiple_of((index // groups) * SUB_ROWS, SUB_ROWS)
        col_at = pl.multiple_of((index % groups) * LANES, LANES)
        tx = txy_ref[0, pl.ds(row_at, SUB_ROWS), :]
        ty = txy_ref[1, pl.ds(row_at, SUB_ROWS), :]
        sx = sxy_ref[pl.ds(0, 1), pl.ds(col_at, LANES)]
        sy = sxy_ref[pl.ds(1, 1), pl.ds(col_at, LANES)]
        delta_x = tx - sx
        delta_y = ty - sy
        radius = jnp.sqrt(delta_x * delta_x + delta_y * delta_y + 0.25)
        decay_rate = jnp.exp(-0.005 * radius)
        cos_part, sin_part = cos_and_sin(1.5 * radius)
        step_re = decay_rate * cos_part
        step_im = decay_rate * sin_part

        def coef(n):
            return (coef_ref[pl.ds(n, 1), pl.ds(col_at, LANES)],
                    coef_ref[pl.ds(terms + n, 1), pl.ds(col_at, LANES)])

        last_re, last_im = coef(terms - 1)
        total_re = jnp.broadcast_to(last_re, radius.shape)
        total_im = jnp.broadcast_to(last_im, radius.shape)
        for degree in range(terms - 2, -1, -1):
            c_re, c_im = coef(degree)
            next_re = total_re * step_re - total_im * step_im + c_re
            next_im = total_re * step_im + total_im * step_re + c_im
            total_re, total_im = next_re, next_im
        series_re = total_re * step_re - total_im * step_im
        series_im = total_re * step_im + total_im * step_re
        re_scr[pl.ds(row_at, SUB_ROWS), pl.ds(col_at, LANES)] = (1.0 / radius + series_re).astype(jnp.bfloat16)
        im_scr[pl.ds(row_at, SUB_ROWS), pl.ds(col_at, LANES)] = series_im.astype(jnp.bfloat16)
        return carry

    lax.fori_loop(0, (rows // SUB_ROWS) * groups, one_sub, 0, unroll=2)
    probe = probe_ref[...]
    rank = probe.shape[1]
    out_ref[:, :rank] += jnp.dot(re_scr[...], probe, preferred_element_type=jnp.float32)
    out_ref[:, rank:] += jnp.dot(im_scr[...], probe, preferred_element_type=jnp.float32)


def sketch_pallas(target_xy, source_xy, series_coef, body_of, probe_matrix):
    rows = target_xy.shape[1]
    sources = source_xy.shape[1]
    rank = probe_matrix.shape[1]
    col_block = min(COL_BLOCK, sources)
    txy = jnp.broadcast_to(target_xy[:, :, None], (2, rows, LANES))
    table = series_coef.reshape(-1, series_coef.shape[2])
    return pl.pallas_call(
        sketch_kernel,
        grid=(sources // col_block,),
        in_specs=[
            pl.BlockSpec((2, rows, LANES), lambda j: (0, 0, 0)),
            pl.BlockSpec((2, col_block), lambda j: (0, j)),
            pl.BlockSpec(table.shape, lambda j: (0, 0)),
            pl.BlockSpec((1, col_block), lambda j: (0, j)),
            pl.BlockSpec((col_block, rank), lambda j: (j, 0)),
        ],
        out_specs=pl.BlockSpec((rows, 2 * rank), lambda j: (0, 0)),
        out_shape=jax.ShapeDtypeStruct((rows, 2 * rank), jnp.float32),
        scratch_shapes=[pltpu.VMEM((table.shape[0], col_block), jnp.float32),
                        pltpu.VMEM((rows, col_block), jnp.bfloat16),
                        pltpu.VMEM((rows, col_block), jnp.bfloat16)],
    )(txy, source_xy, table, body_of.reshape(1, sources), probe_matrix)


def factor_kernel(gram_ref, rows_ref, upper_ref, basis_ref, inverse_ref):
    size = gram_ref.shape[0]
    upper_ref[...] = gram_ref[...]
    rows = lax.broadcasted_iota(jnp.int32, (size, size), 0)
    cols = lax.broadcasted_iota(jnp.int32, (size, size), 1)
    inverse_ref[...] = jnp.where(rows == cols, 1.0, 0.0).astype(jnp.float32)
    lane = lax.broadcasted_iota(jnp.int32, (1, size), 1)
    sublane = lax.broadcasted_iota(jnp.int32, (size, 1), 0)

    def step(j, carry):
        left = upper_ref[...]
        row_left = upper_ref[pl.ds(j, 1), :]
        row_right = inverse_ref[pl.ds(j, 1), :]
        pivot = jnp.sum(jnp.where(lane == j, row_left, 0.0), axis=1, keepdims=True)
        scale = 1.0 / jnp.sqrt(pivot)
        pivot_left = jnp.where(lane >= j, row_left * scale, 0.0)
        pivot_right = row_right * scale
        column = jnp.sum(jnp.where(cols == j, left, 0.0), axis=1, keepdims=True)
        multiplier = jnp.where(sublane > j, column * scale, 0.0)
        upper_ref[...] = left - multiplier * pivot_left
        inverse_ref[...] = inverse_ref[...] - multiplier * pivot_right
        upper_ref[pl.ds(j, 1), :] = pivot_left
        inverse_ref[pl.ds(j, 1), :] = pivot_right
        return carry

    lax.fori_loop(0, size, step, 0)
    upper_ref[...] = jnp.where(rows <= cols, upper_ref[...], 0.0)
    inverse = inverse_ref[...]
    for half in range(rows_ref.shape[1] // size):
        basis_ref[:, half * size : (half + 1) * size] = lax.dot_general(
            rows_ref[:, half * size : (half + 1) * size],
            inverse,
            (((1,), (1,)), ((), ())),
            precision=lax.Precision.HIGHEST,
            preferred_element_type=jnp.float32,
        )


def factor_pallas(gram, own_rows):
    size = gram.shape[0]
    return pl.pallas_call(
        factor_kernel,
        out_shape=(jax.ShapeDtypeStruct((size, size), jnp.float32),
                   jax.ShapeDtypeStruct(own_rows.shape, jnp.float32)),
        scratch_shapes=[pltpu.VMEM((size, size), jnp.float32)],
    )(gram, own_rows)


def in_blocks(array, dim, count):
    shape = array.shape
    tiles = array.reshape(*shape[:dim], count, shape[dim] // count, *shape[dim + 1 :])
    return jnp.moveaxis(tiles, dim, 0)


def sent_and_summed(array, axis, dim):
    tiles = in_blocks(array, dim, lax.axis_size(axis))
    arrived = lax.all_to_all(tiles, axis, split_axis=0, concat_axis=0, tiled=True)
    return arrived.sum(axis=0)


def from_everyone(array, axis):
    copies = jnp.broadcast_to(array, (lax.axis_size(axis), *array.shape))
    return lax.all_to_all(copies, axis, split_axis=0, concat_axis=0, tiled=True)


def of_everyone(array, axis):
    everything = from_everyone(array, axis)
    return jnp.sum(everything, axis=0)


def panel_series(rows_xy, cols_xy, coef_re, coef_im):
    delta_x = rows_xy[0][:, None] - cols_xy[0][None, :]
    delta_y = rows_xy[1][:, None] - cols_xy[1][None, :]
    radius = jnp.sqrt(delta_x * delta_x + delta_y * delta_y + 0.25)
    decay_rate = jnp.exp(-0.005 * radius)
    step_re = decay_rate * jnp.cos(1.5 * radius)
    step_im = decay_rate * jnp.sin(1.5 * radius)
    term_count = coef_re.shape[0]
    total_re = jnp.broadcast_to(coef_re[term_count - 1][None, :], radius.shape)
    total_im = jnp.broadcast_to(coef_im[term_count - 1][None, :], radius.shape)
    for degree in range(term_count - 2, -1, -1):
        next_re = total_re * step_re - total_im * step_im + coef_re[degree][None, :]
        next_im = total_re * step_im + total_im * step_re + coef_im[degree][None, :]
        total_re, total_im = (next_re, next_im)
    series_re = total_re * step_re - total_im * step_im
    series_im = total_re * step_im + total_im * step_re
    tile_re = (1.0 / radius + series_re).astype(jnp.bfloat16)
    tile_im = series_im.astype(jnp.bfloat16)
    return (tile_re, tile_im)


def sketch_rows(target_xy, source_xy, picked, probe_matrix, row_count):
    source_count = probe_matrix.shape[0]
    block_width = math.gcd(source_count, 1024)
    blocks = source_count // block_width
    rank_width = probe_matrix.shape[1]

    def add_block(block_index, totals):
        block_start = block_index * block_width
        xy_block = lax.dynamic_slice_in_dim(source_xy, block_start, block_width, 1)
        coef_block = lax.dynamic_slice_in_dim(picked, block_start, block_width, 1)
        probe_block = lax.dynamic_slice_in_dim(probe_matrix, block_start, block_width, 0)
        tile_re, tile_im = panel_series(
            target_xy, xy_block, coef_block[:NTERMS], coef_block[NTERMS:]
        )
        part_re = jnp.dot(tile_re, probe_block, preferred_element_type=jnp.float32)
        part_im = jnp.dot(tile_im, probe_block, preferred_element_type=jnp.float32)
        return totals + jnp.concatenate([part_re, part_im], axis=1)

    start_totals = jnp.zeros((row_count, 2 * rank_width), jnp.float32)
    return lax.fori_loop(0, blocks, add_block, start_totals)


def gram_of(rows_part, scale_rows):
    rank_width = rows_part.shape[1] // 2
    stacked = rows_part.reshape(-1, rank_width)
    return jnp.dot(stacked.T, stacked, precision=lax.Precision.HIGHEST) / scale_rows


def pick_coefficients(series_coef, body_of):
    bodies = series_coef.shape[2]
    one_hot = (jnp.arange(bodies, dtype=jnp.int32)[:, None] == body_of[None, :]).astype(
        jnp.bfloat16
    )
    table = series_coef.reshape(-1, bodies)
    high_part = table.astype(jnp.bfloat16)
    rest_one = table - high_part.astype(jnp.float32)
    middle_part = rest_one.astype(jnp.bfloat16)
    low_part = (rest_one - middle_part.astype(jnp.float32)).astype(jnp.bfloat16)
    picked = jnp.dot(high_part, one_hot, preferred_element_type=jnp.float32)
    picked = picked + jnp.dot(middle_part, one_hot, preferred_element_type=jnp.float32)
    return picked + jnp.dot(low_part, one_hot, preferred_element_type=jnp.float32)


def per_device(target_xy, source_xy, body_of, series_coef, probe_matrix, row_weight):
    rank_width = probe_matrix.shape[1]
    rows_all = target_xy.shape[1]
    own_count = rows_all // lax.axis_size("src")
    scale_rows = float(2 * rows_all * lax.axis_size("tgt"))
    own_start = lax.axis_index("src") * own_count
    own_sum = sent_and_summed(
        sketch_pallas(target_xy, source_xy, series_coef, body_of, probe_matrix),
        "src",
        0,
    )
    own_weight = lax.dynamic_slice_in_dim(row_weight, own_start, own_count, 0)
    own_rows = own_sum * own_weight[:, None]
    local_gram = gram_of(own_rows, scale_rows)
    gram_piece = sent_and_summed(local_gram, "src", 0)
    gram_piece = of_everyone(gram_piece, "tgt")
    full_gram = from_everyone(gram_piece, "src").reshape(rank_width, rank_width)
    upper_factor, basis_rows = factor_pallas(full_gram, own_rows)
    return (basis_rows, upper_factor)


def solution(mesh):
    return jax.shard_map(
        per_device,
        mesh=mesh,
        in_specs=(P(None, "tgt"), P(None, "src"), P("src"), P(), P("src", None), P("tgt")),
        out_specs=(P(("tgt", "src"), None), P()),
        check_vma=False,
    )
```

```python
import math

import jax
import jax.numpy as jnp
from jax import lax
from jax.experimental import pallas as pl
from jax.experimental.pallas import tpu as pltpu
from jax.sharding import PartitionSpec as P

NTERMS = 32
SUB_ROWS = 64
LANES = 128
COL_BLOCK = 512


def cos_and_sin(angle):
    quarter = jnp.floor(angle * 0.6366197723675814 + 0.5)
    rest = angle - quarter * 1.5703125
    rest = rest - quarter * 4.837512969970703125e-4
    rest = rest - quarter * 7.54978995489188216e-8
    square = rest * rest
    sin_rest = rest + rest * square * (
        -1.6666654611e-1 + square * (8.3321608736e-3 + square * -1.9515295891e-4)
    )
    cos_rest = (1.0 - 0.5 * square) + square * square * (
        4.166664568298827e-2 + square * (-1.388731625493765e-3 + square * 2.443315711809948e-5)
    )
    turn = quarter.astype(jnp.int32)
    swap = (turn & 1) == 1
    sin_value = jnp.where(swap, cos_rest, sin_rest)
    cos_value = jnp.where(swap, sin_rest, cos_rest)
    sin_value = jnp.where((turn & 2) == 2, -sin_value, sin_value)
    cos_value = jnp.where(((turn + 1) & 2) == 2, -cos_value, cos_value)
    return cos_value, sin_value


def sketch_kernel(target_ref, sxy_ref, table_ref, body_ref, probe_ref, out_ref, txy_ref, coef_ref, re_scr, im_scr):
    col_step = pl.program_id(0)
    rows = re_scr.shape[0]
    groups = re_scr.shape[1] // LANES
    terms = coef_ref.shape[0] // 2

    @pl.when(col_step == 0)
    def _():
        out_ref[...] = jnp.zeros_like(out_ref)
        tile = jnp.zeros((8, rows), jnp.float32)
        tile = jnp.where(lax.broadcasted_iota(jnp.int32, (8, rows), 0) == 0, target_ref[0:1, :], tile)
        tile = jnp.where(lax.broadcasted_iota(jnp.int32, (8, rows), 0) == 1, target_ref[1:2, :], tile)
        columns = jnp.transpose(tile)
        txy_ref[0] = jnp.broadcast_to(columns[:, 0:1], (rows, LANES))
        txy_ref[1] = jnp.broadcast_to(columns[:, 1:2], (rows, LANES))

    table = table_ref[...]
    bodies = table.shape[1]
    one_hot = (
        lax.broadcasted_iota(jnp.int32, (bodies, body_ref.shape[1]), 0) == body_ref[...]
    ).astype(jnp.bfloat16)
    high_part = table.astype(jnp.bfloat16)
    rest_one = table - high_part.astype(jnp.float32)
    middle_part = rest_one.astype(jnp.bfloat16)
    low_part = (rest_one - middle_part.astype(jnp.float32)).astype(jnp.bfloat16)
    picked = jnp.dot(high_part, one_hot, preferred_element_type=jnp.float32)
    picked = picked + jnp.dot(middle_part, one_hot, preferred_element_type=jnp.float32)
    coef_ref[...] = picked + jnp.dot(low_part, one_hot, preferred_element_type=jnp.float32)

    def one_sub(index, carry):
        row_at = pl.multiple_of((index // groups) * SUB_ROWS, SUB_ROWS)
        col_at = pl.multiple_of((index % groups) * LANES, LANES)
        tx = txy_ref[0, pl.ds(row_at, SUB_ROWS), :]
        ty = txy_ref[1, pl.ds(row_at, SUB_ROWS), :]
        sx = sxy_ref[pl.ds(0, 1), pl.ds(col_at, LANES)]
        sy = sxy_ref[pl.ds(1, 1), pl.ds(col_at, LANES)]
        delta_x = tx - sx
        delta_y = ty - sy
        radius = jnp.sqrt(delta_x * delta_x + delta_y * delta_y + 0.25)
        decay_rate = jnp.exp(-0.005 * radius)
        cos_part, sin_part = cos_and_sin(1.5 * radius)
        step_re = decay_rate * cos_part
        step_im = decay_rate * sin_part

        def coef(n):
            return (coef_ref[pl.ds(n, 1), pl.ds(col_at, LANES)],
                    coef_ref[pl.ds(terms + n, 1), pl.ds(col_at, LANES)])

        last_re, last_im = coef(terms - 1)
        total_re = jnp.broadcast_to(last_re, radius.shape)
        total_im = jnp.broadcast_to(last_im, radius.shape)
        for degree in range(terms - 2, -1, -1):
            c_re, c_im = coef(degree)
            next_re = total_re * step_re - total_im * step_im + c_re
            next_im = total_re * step_im + total_im * step_re + c_im
            total_re, total_im = next_re, next_im
        series_re = total_re * step_re - total_im * step_im
        series_im = total_re * step_im + total_im * step_re
        re_scr[pl.ds(row_at, SUB_ROWS), pl.ds(col_at, LANES)] = (1.0 / radius + series_re).astype(jnp.bfloat16)
        im_scr[pl.ds(row_at, SUB_ROWS), pl.ds(col_at, LANES)] = series_im.astype(jnp.bfloat16)
        return carry

    lax.fori_loop(0, (rows // SUB_ROWS) * groups, one_sub, 0, unroll=2)
    probe = probe_ref[...]
    rank = probe.shape[1]
    out_ref[:, :rank] += jnp.dot(re_scr[...], probe, preferred_element_type=jnp.float32)
    out_ref[:, rank:] += jnp.dot(im_scr[...], probe, preferred_element_type=jnp.float32)


def sketch_pallas(target_xy, source_xy, series_coef, body_of, probe_matrix):
    rows = target_xy.shape[1]
    sources = source_xy.shape[1]
    rank = probe_matrix.shape[1]
    col_block = min(COL_BLOCK, sources)
    table = series_coef.reshape(-1, series_coef.shape[2])
    return pl.pallas_call(
        sketch_kernel,
        grid=(sources // col_block,),
        in_specs=[
            pl.BlockSpec((2, rows), lambda j: (0, 0)),
            pl.BlockSpec((2, col_block), lambda j: (0, j)),
            pl.BlockSpec(table.shape, lambda j: (0, 0)),
            pl.BlockSpec((1, col_block), lambda j: (0, j)),
            pl.BlockSpec((col_block, rank), lambda j: (j, 0)),
        ],
        out_specs=pl.BlockSpec((rows, 2 * rank), lambda j: (0, 0)),
        out_shape=jax.ShapeDtypeStruct((rows, 2 * rank), jnp.float32),
        scratch_shapes=[pltpu.VMEM((2, rows, LANES), jnp.float32),
                        pltpu.VMEM((table.shape[0], col_block), jnp.float32),
                        pltpu.VMEM((rows, col_block), jnp.bfloat16),
                        pltpu.VMEM((rows, col_block), jnp.bfloat16)],
    )(target_xy, source_xy, table, body_of.reshape(1, sources), probe_matrix)


def factor_kernel(gram_ref, rows_ref, upper_ref, basis_ref, inverse_ref):
    size = gram_ref.shape[0]
    upper_ref[...] = gram_ref[...]
    rows = lax.broadcasted_iota(jnp.int32, (size, size), 0)
    cols = lax.broadcasted_iota(jnp.int32, (size, size), 1)
    inverse_ref[...] = jnp.where(rows == cols, 1.0, 0.0).astype(jnp.float32)
    lane = lax.broadcasted_iota(jnp.int32, (1, size), 1)
    sublane = lax.broadcasted_iota(jnp.int32, (size, 1), 0)

    def step(j, carry):
        left = upper_ref[...]
        row_left = upper_ref[pl.ds(j, 1), :]
        row_right = inverse_ref[pl.ds(j, 1), :]
        pivot = jnp.sum(jnp.where(lane == j, row_left, 0.0), axis=1, keepdims=True)
        scale = 1.0 / jnp.sqrt(pivot)
        pivot_left = jnp.where(lane >= j, row_left * scale, 0.0)
        pivot_right = row_right * scale
        column = jnp.sum(jnp.where(cols == j, left, 0.0), axis=1, keepdims=True)
        multiplier = jnp.where(sublane > j, column * scale, 0.0)
        upper_ref[...] = left - multiplier * pivot_left
        inverse_ref[...] = inverse_ref[...] - multiplier * pivot_right
        upper_ref[pl.ds(j, 1), :] = pivot_left
        inverse_ref[pl.ds(j, 1), :] = pivot_right
        return carry

    lax.fori_loop(0, size, step, 0)
    upper_ref[...] = jnp.where(rows <= cols, upper_ref[...], 0.0)
    inverse = inverse_ref[...]
    for half in range(rows_ref.shape[1] // size):
        basis_ref[:, half * size : (half + 1) * size] = lax.dot_general(
            rows_ref[:, half * size : (half + 1) * size],
            inverse,
            (((1,), (1,)), ((), ())),
            precision=lax.Precision.HIGHEST,
            preferred_element_type=jnp.float32,
        )


def factor_pallas(gram, own_rows):
    size = gram.shape[0]
    return pl.pallas_call(
        factor_kernel,
        out_shape=(jax.ShapeDtypeStruct((size, size), jnp.float32),
                   jax.ShapeDtypeStruct(own_rows.shape, jnp.float32)),
        scratch_shapes=[pltpu.VMEM((size, size), jnp.float32)],
    )(gram, own_rows)


def in_blocks(array, dim, count):
    shape = array.shape
    tiles = array.reshape(*shape[:dim], count, shape[dim] // count, *shape[dim + 1 :])
    return jnp.moveaxis(tiles, dim, 0)


def sent_and_summed(array, axis, dim):
    tiles = in_blocks(array, dim, lax.axis_size(axis))
    arrived = lax.all_to_all(tiles, axis, split_axis=0, concat_axis=0, tiled=True)
    return arrived.sum(axis=0)


def from_everyone(array, axis):
    copies = jnp.broadcast_to(array, (lax.axis_size(axis), *array.shape))
    return lax.all_to_all(copies, axis, split_axis=0, concat_axis=0, tiled=True)


def of_everyone(array, axis):
    everything = from_everyone(array, axis)
    return jnp.sum(everything, axis=0)


def panel_series(rows_xy, cols_xy, coef_re, coef_im):
    delta_x = rows_xy[0][:, None] - cols_xy[0][None, :]
    delta_y = rows_xy[1][:, None] - cols_xy[1][None, :]
    radius = jnp.sqrt(delta_x * delta_x + delta_y * delta_y + 0.25)
    decay_rate = jnp.exp(-0.005 * radius)
    step_re = decay_rate * jnp.cos(1.5 * radius)
    step_im = decay_rate * jnp.sin(1.5 * radius)
    term_count = coef_re.shape[0]
    total_re = jnp.broadcast_to(coef_re[term_count - 1][None, :], radius.shape)
    total_im = jnp.broadcast_to(coef_im[term_count - 1][None, :], radius.shape)
    for degree in range(term_count - 2, -1, -1):
        next_re = total_re * step_re - total_im * step_im + coef_re[degree][None, :]
        next_im = total_re * step_im + total_im * step_re + coef_im[degree][None, :]
        total_re, total_im = (next_re, next_im)
    series_re = total_re * step_re - total_im * step_im
    series_im = total_re * step_im + total_im * step_re
    tile_re = (1.0 / radius + series_re).astype(jnp.bfloat16)
    tile_im = series_im.astype(jnp.bfloat16)
    return (tile_re, tile_im)


def sketch_rows(target_xy, source_xy, picked, probe_matrix, row_count):
    source_count = probe_matrix.shape[0]
    block_width = math.gcd(source_count, 1024)
    blocks = source_count // block_width
    rank_width = probe_matrix.shape[1]

    def add_block(block_index, totals):
        block_start = block_index * block_width
        xy_block = lax.dynamic_slice_in_dim(source_xy, block_start, block_width, 1)
        coef_block = lax.dynamic_slice_in_dim(picked, block_start, block_width, 1)
        probe_block = lax.dynamic_slice_in_dim(probe_matrix, block_start, block_width, 0)
        tile_re, tile_im = panel_series(
            target_xy, xy_block, coef_block[:NTERMS], coef_block[NTERMS:]
        )
        part_re = jnp.dot(tile_re, probe_block, preferred_element_type=jnp.float32)
        part_im = jnp.dot(tile_im, probe_block, preferred_element_type=jnp.float32)
        return totals + jnp.concatenate([part_re, part_im], axis=1)

    start_totals = jnp.zeros((row_count, 2 * rank_width), jnp.float32)
    return lax.fori_loop(0, blocks, add_block, start_totals)


def gram_of(rows_part, scale_rows):
    rank_width = rows_part.shape[1] // 2
    stacked = rows_part.reshape(-1, rank_width)
    return jnp.dot(stacked.T, stacked, precision=lax.Precision.HIGHEST) / scale_rows


def pick_coefficients(series_coef, body_of):
    bodies = series_coef.shape[2]
    one_hot = (jnp.arange(bodies, dtype=jnp.int32)[:, None] == body_of[None, :]).astype(
        jnp.bfloat16
    )
    table = series_coef.reshape(-1, bodies)
    high_part = table.astype(jnp.bfloat16)
    rest_one = table - high_part.astype(jnp.float32)
    middle_part = rest_one.astype(jnp.bfloat16)
    low_part = (rest_one - middle_part.astype(jnp.float32)).astype(jnp.bfloat16)
    picked = jnp.dot(high_part, one_hot, preferred_element_type=jnp.float32)
    picked = picked + jnp.dot(middle_part, one_hot, preferred_element_type=jnp.float32)
    return picked + jnp.dot(low_part, one_hot, preferred_element_type=jnp.float32)


def per_device(target_xy, source_xy, body_of, series_coef, probe_matrix, row_weight):
    rank_width = probe_matrix.shape[1]
    rows_all = target_xy.shape[1]
    own_count = rows_all // lax.axis_size("src")
    scale_rows = float(2 * rows_all * lax.axis_size("tgt"))
    own_start = lax.axis_index("src") * own_count
    own_sum = sent_and_summed(
        sketch_pallas(target_xy, source_xy, series_coef, body_of, probe_matrix),
        "src",
        0,
    )
    own_weight = lax.dynamic_slice_in_dim(row_weight, own_start, own_count, 0)
    own_rows = own_sum * own_weight[:, None]
    local_gram = gram_of(own_rows, scale_rows)
    gram_piece = sent_and_summed(local_gram, "src", 0)
    gram_piece = of_everyone(gram_piece, "tgt")
    full_gram = from_everyone(gram_piece, "src").reshape(rank_width, rank_width)
    upper_factor, basis_rows = factor_pallas(full_gram, own_rows)
    return (basis_rows, upper_factor)


def solution(mesh):
    return jax.shard_map(
        per_device,
        mesh=mesh,
        in_specs=(P(None, "tgt"), P(None, "src"), P("src"), P(), P("src", None), P("tgt")),
        out_specs=(P(("tgt", "src"), None), P()),
        check_vma=False,
    )
```

```python
import functools
import math

import jax
import jax.numpy as jnp
from jax import lax
from jax.experimental import pallas as pl
from jax.experimental.pallas import tpu as pltpu
from jax.sharding import PartitionSpec as P

NTERMS = 32
SUB_ROWS = 64
LANES = 128
COL_BLOCK = 512


def cos_and_sin(angle):
    quarter = jnp.floor(angle * 0.6366197723675814 + 0.5)
    rest = angle - quarter * 1.5703125
    rest = rest - quarter * 4.837512969970703125e-4
    rest = rest - quarter * 7.54978995489188216e-8
    square = rest * rest
    sin_rest = rest + rest * square * (
        -1.6666654611e-1 + square * (8.3321608736e-3 + square * -1.9515295891e-4)
    )
    cos_rest = (1.0 - 0.5 * square) + square * square * (
        4.166664568298827e-2 + square * (-1.388731625493765e-3 + square * 2.443315711809948e-5)
    )
    turn = quarter.astype(jnp.int32)
    swap = (turn & 1) == 1
    sin_value = jnp.where(swap, cos_rest, sin_rest)
    cos_value = jnp.where(swap, sin_rest, cos_rest)
    sin_value = jnp.where((turn & 2) == 2, -sin_value, sin_value)
    cos_value = jnp.where(((turn + 1) & 2) == 2, -cos_value, cos_value)
    return cos_value, sin_value


def sketch_kernel(target_ref, sxy_ref, table_ref, body_ref, probe_ref, out_ref, txy_ref, coef_ref, re_scr, im_scr, *, part, parts, owners):
    col_step = pl.program_id(0)
    rows = re_scr.shape[0]
    groups = re_scr.shape[1] // LANES
    terms = coef_ref.shape[0] // 2

    @pl.when(col_step == 0)
    def _():
        out_ref[...] = jnp.zeros_like(out_ref)
        all_rows = target_ref.shape[1]
        tile = jnp.zeros((8, all_rows), jnp.float32)
        tile = jnp.where(lax.broadcasted_iota(jnp.int32, (8, all_rows), 0) == 0, target_ref[0:1, :], tile)
        tile = jnp.where(lax.broadcasted_iota(jnp.int32, (8, all_rows), 0) == 1, target_ref[1:2, :], tile)
        columns = jnp.transpose(tile)
        piece = all_rows // (owners * parts)
        for block in range(owners):
            start = block * piece * parts + part * piece
            picked_rows = columns[start : start + piece, :]
            txy_ref[0, block * piece : (block + 1) * piece, :] = jnp.broadcast_to(picked_rows[:, 0:1], (piece, LANES))
            txy_ref[1, block * piece : (block + 1) * piece, :] = jnp.broadcast_to(picked_rows[:, 1:2], (piece, LANES))

    table = table_ref[...]
    bodies = table.shape[1]
    one_hot = (
        lax.broadcasted_iota(jnp.int32, (bodies, body_ref.shape[1]), 0) == body_ref[...]
    ).astype(jnp.bfloat16)
    high_part = table.astype(jnp.bfloat16)
    rest_one = table - high_part.astype(jnp.float32)
    middle_part = rest_one.astype(jnp.bfloat16)
    low_part = (rest_one - middle_part.astype(jnp.float32)).astype(jnp.bfloat16)
    picked = jnp.dot(high_part, one_hot, preferred_element_type=jnp.float32)
    picked = picked + jnp.dot(middle_part, one_hot, preferred_element_type=jnp.float32)
    coef_ref[...] = picked + jnp.dot(low_part, one_hot, preferred_element_type=jnp.float32)

    def one_sub(index, carry):
        row_at = pl.multiple_of((index // groups) * SUB_ROWS, SUB_ROWS)
        col_at = pl.multiple_of((index % groups) * LANES, LANES)
        tx = txy_ref[0, pl.ds(row_at, SUB_ROWS), :]
        ty = txy_ref[1, pl.ds(row_at, SUB_ROWS), :]
        sx = sxy_ref[pl.ds(0, 1), pl.ds(col_at, LANES)]
        sy = sxy_ref[pl.ds(1, 1), pl.ds(col_at, LANES)]
        delta_x = tx - sx
        delta_y = ty - sy
        radius = jnp.sqrt(delta_x * delta_x + delta_y * delta_y + 0.25)
        decay_rate = jnp.exp(-0.005 * radius)
        cos_part, sin_part = cos_and_sin(1.5 * radius)
        step_re = decay_rate * cos_part
        step_im = decay_rate * sin_part

        def coef(n):
            return (coef_ref[pl.ds(n, 1), pl.ds(col_at, LANES)],
                    coef_ref[pl.ds(terms + n, 1), pl.ds(col_at, LANES)])

        last_re, last_im = coef(terms - 1)
        total_re = jnp.broadcast_to(last_re, radius.shape)
        total_im = jnp.broadcast_to(last_im, radius.shape)
        for degree in range(terms - 2, -1, -1):
            c_re, c_im = coef(degree)
            next_re = total_re * step_re - total_im * step_im + c_re
            next_im = total_re * step_im + total_im * step_re + c_im
            total_re, total_im = next_re, next_im
        series_re = total_re * step_re - total_im * step_im
        series_im = total_re * step_im + total_im * step_re
        re_scr[pl.ds(row_at, SUB_ROWS), pl.ds(col_at, LANES)] = (1.0 / radius + series_re).astype(jnp.bfloat16)
        im_scr[pl.ds(row_at, SUB_ROWS), pl.ds(col_at, LANES)] = series_im.astype(jnp.bfloat16)
        return carry

    lax.fori_loop(0, (rows // SUB_ROWS) * groups, one_sub, 0, unroll=2)
    probe = probe_ref[...]
    rank = probe.shape[1]
    out_ref[:, :rank] += jnp.dot(re_scr[...], probe, preferred_element_type=jnp.float32)
    out_ref[:, rank:] += jnp.dot(im_scr[...], probe, preferred_element_type=jnp.float32)


def sketch_pallas(target_xy, source_xy, series_coef, body_of, probe_matrix, part, parts, owners):
    rows = target_xy.shape[1] // parts
    sources = source_xy.shape[1]
    rank = probe_matrix.shape[1]
    col_block = min(COL_BLOCK, sources)
    table = series_coef.reshape(-1, series_coef.shape[2])
    return pl.pallas_call(
        functools.partial(sketch_kernel, part=part, parts=parts, owners=owners),
        grid=(sources // col_block,),
        in_specs=[
            pl.BlockSpec((2, target_xy.shape[1]), lambda j: (0, 0)),
            pl.BlockSpec((2, col_block), lambda j: (0, j)),
            pl.BlockSpec(table.shape, lambda j: (0, 0)),
            pl.BlockSpec((1, col_block), lambda j: (0, j)),
            pl.BlockSpec((col_block, rank), lambda j: (j, 0)),
        ],
        out_specs=pl.BlockSpec((rows, 2 * rank), lambda j: (0, 0)),
        out_shape=jax.ShapeDtypeStruct((rows, 2 * rank), jnp.float32),
        scratch_shapes=[pltpu.VMEM((2, rows, LANES), jnp.float32),
                        pltpu.VMEM((table.shape[0], col_block), jnp.float32),
                        pltpu.VMEM((rows, col_block), jnp.bfloat16),
                        pltpu.VMEM((rows, col_block), jnp.bfloat16)],
    )(target_xy, source_xy, table, body_of.reshape(1, sources), probe_matrix)


def factor_kernel(gram_ref, rows_ref, upper_ref, basis_ref, inverse_ref):
    size = gram_ref.shape[0]
    upper_ref[...] = gram_ref[...]
    rows = lax.broadcasted_iota(jnp.int32, (size, size), 0)
    cols = lax.broadcasted_iota(jnp.int32, (size, size), 1)
    inverse_ref[...] = jnp.where(rows == cols, 1.0, 0.0).astype(jnp.float32)
    lane = lax.broadcasted_iota(jnp.int32, (1, size), 1)
    sublane = lax.broadcasted_iota(jnp.int32, (size, 1), 0)

    def step(j, carry):
        left = upper_ref[...]
        row_left = upper_ref[pl.ds(j, 1), :]
        row_right = inverse_ref[pl.ds(j, 1), :]
        pivot = jnp.sum(jnp.where(lane == j, row_left, 0.0), axis=1, keepdims=True)
        scale = 1.0 / jnp.sqrt(pivot)
        pivot_left = jnp.where(lane >= j, row_left * scale, 0.0)
        pivot_right = row_right * scale
        column = jnp.sum(jnp.where(cols == j, left, 0.0), axis=1, keepdims=True)
        multiplier = jnp.where(sublane > j, column * scale, 0.0)
        upper_ref[...] = left - multiplier * pivot_left
        inverse_ref[...] = inverse_ref[...] - multiplier * pivot_right
        upper_ref[pl.ds(j, 1), :] = pivot_left
        inverse_ref[pl.ds(j, 1), :] = pivot_right
        return carry

    lax.fori_loop(0, size, step, 0)
    upper_ref[...] = jnp.where(rows <= cols, upper_ref[...], 0.0)
    inverse = inverse_ref[...]
    for half in range(rows_ref.shape[1] // size):
        basis_ref[:, half * size : (half + 1) * size] = lax.dot_general(
            rows_ref[:, half * size : (half + 1) * size],
            inverse,
            (((1,), (1,)), ((), ())),
            precision=lax.Precision.HIGHEST,
            preferred_element_type=jnp.float32,
        )


def factor_pallas(gram, own_rows):
    size = gram.shape[0]
    return pl.pallas_call(
        factor_kernel,
        out_shape=(jax.ShapeDtypeStruct((size, size), jnp.float32),
                   jax.ShapeDtypeStruct(own_rows.shape, jnp.float32)),
        scratch_shapes=[pltpu.VMEM((size, size), jnp.float32)],
    )(gram, own_rows)


def in_blocks(array, dim, count):
    shape = array.shape
    tiles = array.reshape(*shape[:dim], count, shape[dim] // count, *shape[dim + 1 :])
    return jnp.moveaxis(tiles, dim, 0)


def sent_and_summed(array, axis, dim):
    tiles = in_blocks(array, dim, lax.axis_size(axis))
    arrived = lax.all_to_all(tiles, axis, split_axis=0, concat_axis=0, tiled=True)
    return arrived.sum(axis=0)


def from_everyone(array, axis):
    copies = jnp.broadcast_to(array, (lax.axis_size(axis), *array.shape))
    return lax.all_to_all(copies, axis, split_axis=0, concat_axis=0, tiled=True)


def of_everyone(array, axis):
    everything = from_everyone(array, axis)
    return jnp.sum(everything, axis=0)


def panel_series(rows_xy, cols_xy, coef_re, coef_im):
    delta_x = rows_xy[0][:, None] - cols_xy[0][None, :]
    delta_y = rows_xy[1][:, None] - cols_xy[1][None, :]
    radius = jnp.sqrt(delta_x * delta_x + delta_y * delta_y + 0.25)
    decay_rate = jnp.exp(-0.005 * radius)
    step_re = decay_rate * jnp.cos(1.5 * radius)
    step_im = decay_rate * jnp.sin(1.5 * radius)
    term_count = coef_re.shape[0]
    total_re = jnp.broadcast_to(coef_re[term_count - 1][None, :], radius.shape)
    total_im = jnp.broadcast_to(coef_im[term_count - 1][None, :], radius.shape)
    for degree in range(term_count - 2, -1, -1):
        next_re = total_re * step_re - total_im * step_im + coef_re[degree][None, :]
        next_im = total_re * step_im + total_im * step_re + coef_im[degree][None, :]
        total_re, total_im = (next_re, next_im)
    series_re = total_re * step_re - total_im * step_im
    series_im = total_re * step_im + total_im * step_re
    tile_re = (1.0 / radius + series_re).astype(jnp.bfloat16)
    tile_im = series_im.astype(jnp.bfloat16)
    return (tile_re, tile_im)


def sketch_rows(target_xy, source_xy, picked, probe_matrix, row_count):
    source_count = probe_matrix.shape[0]
    block_width = math.gcd(source_count, 1024)
    blocks = source_count // block_width
    rank_width = probe_matrix.shape[1]

    def add_block(block_index, totals):
        block_start = block_index * block_width
        xy_block = lax.dynamic_slice_in_dim(source_xy, block_start, block_width, 1)
        coef_block = lax.dynamic_slice_in_dim(picked, block_start, block_width, 1)
        probe_block = lax.dynamic_slice_in_dim(probe_matrix, block_start, block_width, 0)
        tile_re, tile_im = panel_series(
            target_xy, xy_block, coef_block[:NTERMS], coef_block[NTERMS:]
        )
        part_re = jnp.dot(tile_re, probe_block, preferred_element_type=jnp.float32)
        part_im = jnp.dot(tile_im, probe_block, preferred_element_type=jnp.float32)
        return totals + jnp.concatenate([part_re, part_im], axis=1)

    start_totals = jnp.zeros((row_count, 2 * rank_width), jnp.float32)
    return lax.fori_loop(0, blocks, add_block, start_totals)


def gram_of(rows_part, scale_rows):
    rank_width = rows_part.shape[1] // 2
    stacked = rows_part.reshape(-1, rank_width)
    return jnp.dot(stacked.T, stacked, precision=lax.Precision.HIGHEST) / scale_rows


def pick_coefficients(series_coef, body_of):
    bodies = series_coef.shape[2]
    one_hot = (jnp.arange(bodies, dtype=jnp.int32)[:, None] == body_of[None, :]).astype(
        jnp.bfloat16
    )
    table = series_coef.reshape(-1, bodies)
    high_part = table.astype(jnp.bfloat16)
    rest_one = table - high_part.astype(jnp.float32)
    middle_part = rest_one.astype(jnp.bfloat16)
    low_part = (rest_one - middle_part.astype(jnp.float32)).astype(jnp.bfloat16)
    picked = jnp.dot(high_part, one_hot, preferred_element_type=jnp.float32)
    picked = picked + jnp.dot(middle_part, one_hot, preferred_element_type=jnp.float32)
    return picked + jnp.dot(low_part, one_hot, preferred_element_type=jnp.float32)


def per_device(target_xy, source_xy, body_of, series_coef, probe_matrix, row_weight):
    rank_width = probe_matrix.shape[1]
    rows_all = target_xy.shape[1]
    own_count = rows_all // lax.axis_size("src")
    scale_rows = float(2 * rows_all * lax.axis_size("tgt"))
    own_start = lax.axis_index("src") * own_count
    parts = 2
    own_sum = jnp.concatenate(
        [
            sent_and_summed(
                sketch_pallas(target_xy, source_xy, series_coef, body_of, probe_matrix, part, parts, lax.axis_size("src")),
                "src",
                0,
            )
            for part in range(parts)
        ],
        axis=0,
    )
    own_weight = lax.dynamic_slice_in_dim(row_weight, own_start, own_count, 0)
    own_rows = own_sum * own_weight[:, None]
    local_gram = gram_of(own_rows, scale_rows)
    gram_piece = sent_and_summed(local_gram, "src", 0)
    gram_piece = of_everyone(gram_piece, "tgt")
    full_gram = from_everyone(gram_piece, "src").reshape(rank_width, rank_width)
    upper_factor, basis_rows = factor_pallas(full_gram, own_rows)
    return (basis_rows, upper_factor)


def solution(mesh):
    return jax.shard_map(
        per_device,
        mesh=mesh,
        in_specs=(P(None, "tgt"), P(None, "src"), P("src"), P(), P("src", None), P("tgt")),
        out_specs=(P(("tgt", "src"), None), P()),
        check_vma=False,
    )
```

```python
import math

import jax
import jax.numpy as jnp
from jax import lax
from jax.experimental import pallas as pl
from jax.experimental.pallas import tpu as pltpu
from jax.sharding import PartitionSpec as P

NTERMS = 32
SUB_ROWS = 64
LANES = 128
COL_BLOCK = 512


def cos_and_sin(angle):
    quarter = jnp.floor(angle * 0.6366197723675814 + 0.5)
    rest = angle - quarter * 1.5703125
    rest = rest - quarter * 4.837512969970703125e-4
    rest = rest - quarter * 7.54978995489188216e-8
    square = rest * rest
    sin_rest = rest + rest * square * (
        -1.6666654611e-1 + square * (8.3321608736e-3 + square * -1.9515295891e-4)
    )
    cos_rest = (1.0 - 0.5 * square) + square * square * (
        4.166664568298827e-2 + square * (-1.388731625493765e-3 + square * 2.443315711809948e-5)
    )
    turn = quarter.astype(jnp.int32)
    swap = (turn & 1) == 1
    sin_value = jnp.where(swap, cos_rest, sin_rest)
    cos_value = jnp.where(swap, sin_rest, cos_rest)
    sin_value = jnp.where((turn & 2) == 2, -sin_value, sin_value)
    cos_value = jnp.where(((turn + 1) & 2) == 2, -cos_value, cos_value)
    return cos_value, sin_value


def sketch_kernel(target_ref, weight_ref, sxy_ref, table_ref, body_ref, probe_ref, out_ref, txy_ref, weight_scr, coef_ref, re_scr, im_scr):
    col_step = pl.program_id(0)
    rows = re_scr.shape[0]
    groups = re_scr.shape[1] // LANES
    terms = coef_ref.shape[0] // 2

    @pl.when(col_step == 0)
    def _():
        out_ref[...] = jnp.zeros_like(out_ref)
        tile = jnp.zeros((8, rows), jnp.float32)
        tile = jnp.where(lax.broadcasted_iota(jnp.int32, (8, rows), 0) == 0, target_ref[0:1, :], tile)
        tile = jnp.where(lax.broadcasted_iota(jnp.int32, (8, rows), 0) == 1, target_ref[1:2, :], tile)
        tile = jnp.where(lax.broadcasted_iota(jnp.int32, (8, rows), 0) == 2, weight_ref[...], tile)
        columns = jnp.transpose(tile)
        txy_ref[0] = jnp.broadcast_to(columns[:, 0:1], (rows, LANES))
        txy_ref[1] = jnp.broadcast_to(columns[:, 1:2], (rows, LANES))
        weight_scr[...] = jnp.broadcast_to(columns[:, 2:3], (rows, LANES))

    table = table_ref[...]
    bodies = table.shape[1]
    one_hot = (
        lax.broadcasted_iota(jnp.int32, (bodies, body_ref.shape[1]), 0) == body_ref[...]
    ).astype(jnp.bfloat16)
    high_part = table.astype(jnp.bfloat16)
    rest_one = table - high_part.astype(jnp.float32)
    middle_part = rest_one.astype(jnp.bfloat16)
    low_part = (rest_one - middle_part.astype(jnp.float32)).astype(jnp.bfloat16)
    picked = jnp.dot(high_part, one_hot, preferred_element_type=jnp.float32)
    picked = picked + jnp.dot(middle_part, one_hot, preferred_element_type=jnp.float32)
    coef_ref[...] = picked + jnp.dot(low_part, one_hot, preferred_element_type=jnp.float32)

    def one_sub(index, carry):
        row_at = pl.multiple_of((index // groups) * SUB_ROWS, SUB_ROWS)
        col_at = pl.multiple_of((index % groups) * LANES, LANES)
        tx = txy_ref[0, pl.ds(row_at, SUB_ROWS), :]
        ty = txy_ref[1, pl.ds(row_at, SUB_ROWS), :]
        sx = sxy_ref[pl.ds(0, 1), pl.ds(col_at, LANES)]
        sy = sxy_ref[pl.ds(1, 1), pl.ds(col_at, LANES)]
        delta_x = tx - sx
        delta_y = ty - sy
        radius = jnp.sqrt(delta_x * delta_x + delta_y * delta_y + 0.25)
        decay_rate = jnp.exp(-0.005 * radius)
        cos_part, sin_part = cos_and_sin(1.5 * radius)
        step_re = decay_rate * cos_part
        step_im = decay_rate * sin_part

        def coef(n):
            return (coef_ref[pl.ds(n, 1), pl.ds(col_at, LANES)],
                    coef_ref[pl.ds(terms + n, 1), pl.ds(col_at, LANES)])

        last_re, last_im = coef(terms - 1)
        total_re = jnp.broadcast_to(last_re, radius.shape)
        total_im = jnp.broadcast_to(last_im, radius.shape)
        for degree in range(terms - 2, -1, -1):
            c_re, c_im = coef(degree)
            next_re = total_re * step_re - total_im * step_im + c_re
            next_im = total_re * step_im + total_im * step_re + c_im
            total_re, total_im = next_re, next_im
        series_re = total_re * step_re - total_im * step_im
        series_im = total_re * step_im + total_im * step_re
        re_scr[pl.ds(row_at, SUB_ROWS), pl.ds(col_at, LANES)] = (1.0 / radius + series_re).astype(jnp.bfloat16)
        im_scr[pl.ds(row_at, SUB_ROWS), pl.ds(col_at, LANES)] = series_im.astype(jnp.bfloat16)
        return carry

    lax.fori_loop(0, (rows // SUB_ROWS) * groups, one_sub, 0, unroll=2)
    probe = probe_ref[...]
    rank = probe.shape[1]
    out_ref[:, :rank] += jnp.dot(re_scr[...], probe, preferred_element_type=jnp.float32)
    out_ref[:, rank:] += jnp.dot(im_scr[...], probe, preferred_element_type=jnp.float32)

    @pl.when(col_step == pl.num_programs(0) - 1)
    def _():
        weight = weight_scr[...]
        out_ref[:, :rank] = out_ref[:, :rank] * weight
        out_ref[:, rank:] = out_ref[:, rank:] * weight


def sketch_pallas(target_xy, row_weight, source_xy, series_coef, body_of, probe_matrix):
    rows = target_xy.shape[1]
    sources = source_xy.shape[1]
    rank = probe_matrix.shape[1]
    col_block = min(COL_BLOCK, sources)
    table = series_coef.reshape(-1, series_coef.shape[2])
    return pl.pallas_call(
        sketch_kernel,
        grid=(sources // col_block,),
        in_specs=[
            pl.BlockSpec((2, rows), lambda j: (0, 0)),
            pl.BlockSpec((1, rows), lambda j: (0, 0)),
            pl.BlockSpec((2, col_block), lambda j: (0, j)),
            pl.BlockSpec(table.shape, lambda j: (0, 0)),
            pl.BlockSpec((1, col_block), lambda j: (0, j)),
            pl.BlockSpec((col_block, rank), lambda j: (j, 0)),
        ],
        out_specs=pl.BlockSpec((rows, 2 * rank), lambda j: (0, 0)),
        out_shape=jax.ShapeDtypeStruct((rows, 2 * rank), jnp.float32),
        scratch_shapes=[pltpu.VMEM((2, rows, LANES), jnp.float32),
                        pltpu.VMEM((rows, LANES), jnp.float32),
                        pltpu.VMEM((table.shape[0], col_block), jnp.float32),
                        pltpu.VMEM((rows, col_block), jnp.bfloat16),
                        pltpu.VMEM((rows, col_block), jnp.bfloat16)],
    )(target_xy, row_weight.reshape(1, rows), source_xy, table, body_of.reshape(1, sources), probe_matrix)


def factor_kernel(gram_ref, rows_ref, upper_ref, basis_ref, inverse_ref):
    size = gram_ref.shape[0]
    upper_ref[...] = gram_ref[...]
    rows = lax.broadcasted_iota(jnp.int32, (size, size), 0)
    cols = lax.broadcasted_iota(jnp.int32, (size, size), 1)
    inverse_ref[...] = jnp.where(rows == cols, 1.0, 0.0).astype(jnp.float32)
    lane = lax.broadcasted_iota(jnp.int32, (1, size), 1)
    sublane = lax.broadcasted_iota(jnp.int32, (size, 1), 0)

    def step(j, carry):
        left = upper_ref[...]
        row_left = upper_ref[pl.ds(j, 1), :]
        row_right = inverse_ref[pl.ds(j, 1), :]
        pivot = jnp.sum(jnp.where(lane == j, row_left, 0.0), axis=1, keepdims=True)
        scale = 1.0 / jnp.sqrt(pivot)
        pivot_left = jnp.where(lane >= j, row_left * scale, 0.0)
        pivot_right = row_right * scale
        column = jnp.sum(jnp.where(cols == j, left, 0.0), axis=1, keepdims=True)
        multiplier = jnp.where(sublane > j, column * scale, 0.0)
        upper_ref[...] = left - multiplier * pivot_left
        inverse_ref[...] = inverse_ref[...] - multiplier * pivot_right
        upper_ref[pl.ds(j, 1), :] = pivot_left
        inverse_ref[pl.ds(j, 1), :] = pivot_right
        return carry

    lax.fori_loop(0, size, step, 0, unroll=2)
    upper_ref[...] = jnp.where(rows <= cols, upper_ref[...], 0.0)
    inverse = inverse_ref[...]
    for half in range(rows_ref.shape[1] // size):
        basis_ref[:, half * size : (half + 1) * size] = lax.dot_general(
            rows_ref[:, half * size : (half + 1) * size],
            inverse,
            (((1,), (1,)), ((), ())),
            precision=lax.Precision.HIGHEST,
            preferred_element_type=jnp.float32,
        )


def factor_pallas(gram, own_rows):
    size = gram.shape[0]
    return pl.pallas_call(
        factor_kernel,
        out_shape=(jax.ShapeDtypeStruct((size, size), jnp.float32),
                   jax.ShapeDtypeStruct(own_rows.shape, jnp.float32)),
        scratch_shapes=[pltpu.VMEM((size, size), jnp.float32)],
    )(gram, own_rows)


def in_blocks(array, dim, count):
    shape = array.shape
    tiles = array.reshape(*shape[:dim], count, shape[dim] // count, *shape[dim + 1 :])
    return jnp.moveaxis(tiles, dim, 0)


def sent_and_summed(array, axis, dim):
    tiles = in_blocks(array, dim, lax.axis_size(axis))
    arrived = lax.all_to_all(tiles, axis, split_axis=0, concat_axis=0, tiled=True)
    return arrived.sum(axis=0)


def from_everyone(array, axis):
    copies = jnp.broadcast_to(array, (lax.axis_size(axis), *array.shape))
    return lax.all_to_all(copies, axis, split_axis=0, concat_axis=0, tiled=True)


def of_everyone(array, axis):
    everything = from_everyone(array, axis)
    return jnp.sum(everything, axis=0)


def panel_series(rows_xy, cols_xy, coef_re, coef_im):
    delta_x = rows_xy[0][:, None] - cols_xy[0][None, :]
    delta_y = rows_xy[1][:, None] - cols_xy[1][None, :]
    radius = jnp.sqrt(delta_x * delta_x + delta_y * delta_y + 0.25)
    decay_rate = jnp.exp(-0.005 * radius)
    step_re = decay_rate * jnp.cos(1.5 * radius)
    step_im = decay_rate * jnp.sin(1.5 * radius)
    term_count = coef_re.shape[0]
    total_re = jnp.broadcast_to(coef_re[term_count - 1][None, :], radius.shape)
    total_im = jnp.broadcast_to(coef_im[term_count - 1][None, :], radius.shape)
    for degree in range(term_count - 2, -1, -1):
        next_re = total_re * step_re - total_im * step_im + coef_re[degree][None, :]
        next_im = total_re * step_im + total_im * step_re + coef_im[degree][None, :]
        total_re, total_im = (next_re, next_im)
    series_re = total_re * step_re - total_im * step_im
    series_im = total_re * step_im + total_im * step_re
    tile_re = (1.0 / radius + series_re).astype(jnp.bfloat16)
    tile_im = series_im.astype(jnp.bfloat16)
    return (tile_re, tile_im)


def sketch_rows(target_xy, source_xy, picked, probe_matrix, row_count):
    source_count = probe_matrix.shape[0]
    block_width = math.gcd(source_count, 1024)
    blocks = source_count // block_width
    rank_width = probe_matrix.shape[1]

    def add_block(block_index, totals):
        block_start = block_index * block_width
        xy_block = lax.dynamic_slice_in_dim(source_xy, block_start, block_width, 1)
        coef_block = lax.dynamic_slice_in_dim(picked, block_start, block_width, 1)
        probe_block = lax.dynamic_slice_in_dim(probe_matrix, block_start, block_width, 0)
        tile_re, tile_im = panel_series(
            target_xy, xy_block, coef_block[:NTERMS], coef_block[NTERMS:]
        )
        part_re = jnp.dot(tile_re, probe_block, preferred_element_type=jnp.float32)
        part_im = jnp.dot(tile_im, probe_block, preferred_element_type=jnp.float32)
        return totals + jnp.concatenate([part_re, part_im], axis=1)

    start_totals = jnp.zeros((row_count, 2 * rank_width), jnp.float32)
    return lax.fori_loop(0, blocks, add_block, start_totals)


def gram_of(rows_part, scale_rows):
    rank_width = rows_part.shape[1] // 2
    stacked = rows_part.reshape(-1, rank_width)
    return jnp.dot(stacked.T, stacked, precision=lax.Precision.HIGHEST) / scale_rows


def pick_coefficients(series_coef, body_of):
    bodies = series_coef.shape[2]
    one_hot = (jnp.arange(bodies, dtype=jnp.int32)[:, None] == body_of[None, :]).astype(
        jnp.bfloat16
    )
    table = series_coef.reshape(-1, bodies)
    high_part = table.astype(jnp.bfloat16)
    rest_one = table - high_part.astype(jnp.float32)
    middle_part = rest_one.astype(jnp.bfloat16)
    low_part = (rest_one - middle_part.astype(jnp.float32)).astype(jnp.bfloat16)
    picked = jnp.dot(high_part, one_hot, preferred_element_type=jnp.float32)
    picked = picked + jnp.dot(middle_part, one_hot, preferred_element_type=jnp.float32)
    return picked + jnp.dot(low_part, one_hot, preferred_element_type=jnp.float32)


def per_device(target_xy, source_xy, body_of, series_coef, probe_matrix, row_weight):
    rank_width = probe_matrix.shape[1]
    rows_all = target_xy.shape[1]
    own_count = rows_all // lax.axis_size("src")
    scale_rows = float(2 * rows_all * lax.axis_size("tgt"))
    own_sum = sent_and_summed(
        sketch_pallas(target_xy, row_weight, source_xy, series_coef, body_of, probe_matrix),
        "src",
        0,
    )
    own_rows = own_sum
    local_gram = gram_of(own_rows, scale_rows)
    gram_piece = sent_and_summed(local_gram, "src", 0)
    gram_piece = of_everyone(gram_piece, "tgt")
    full_gram = from_everyone(gram_piece, "src").reshape(rank_width, rank_width)
    upper_factor, basis_rows = factor_pallas(full_gram, own_rows)
    return (basis_rows, upper_factor)


def solution(mesh):
    return jax.shard_map(
        per_device,
        mesh=mesh,
        in_specs=(P(None, "tgt"), P(None, "src"), P("src"), P(), P("src", None), P("tgt")),
        out_specs=(P(("tgt", "src"), None), P()),
        check_vma=False,
    )
```

```python
import math

import jax
import jax.numpy as jnp
from jax import lax
from jax.experimental import pallas as pl
from jax.experimental.pallas import tpu as pltpu
from jax.sharding import PartitionSpec as P

NTERMS = 32
SUB_ROWS = 64
LANES = 128
COL_BLOCK = 1024


def cos_and_sin(angle):
    quarter = jnp.floor(angle * 0.6366197723675814 + 0.5)
    rest = angle - quarter * 1.5703125
    rest = rest - quarter * 4.837512969970703125e-4
    rest = rest - quarter * 7.54978995489188216e-8
    square = rest * rest
    sin_rest = rest + rest * square * (
        -1.6666654611e-1 + square * (8.3321608736e-3 + square * -1.9515295891e-4)
    )
    cos_rest = (1.0 - 0.5 * square) + square * square * (
        4.166664568298827e-2 + square * (-1.388731625493765e-3 + square * 2.443315711809948e-5)
    )
    turn = quarter.astype(jnp.int32)
    swap = (turn & 1) == 1
    sin_value = jnp.where(swap, cos_rest, sin_rest)
    cos_value = jnp.where(swap, sin_rest, cos_rest)
    sin_value = jnp.where((turn & 2) == 2, -sin_value, sin_value)
    cos_value = jnp.where(((turn + 1) & 2) == 2, -cos_value, cos_value)
    return cos_value, sin_value


def sketch_kernel(target_ref, sxy_ref, table_ref, body_ref, probe_ref, out_ref, txy_ref, coef_ref, re_scr, im_scr):
    col_step = pl.program_id(0)
    rows = re_scr.shape[0]
    groups = re_scr.shape[1] // LANES
    terms = coef_ref.shape[0] // 2

    @pl.when(col_step == 0)
    def _():
        out_ref[...] = jnp.zeros_like(out_ref)
        tile = jnp.zeros((8, rows), jnp.float32)
        tile = jnp.where(lax.broadcasted_iota(jnp.int32, (8, rows), 0) == 0, target_ref[0:1, :], tile)
        tile = jnp.where(lax.broadcasted_iota(jnp.int32, (8, rows), 0) == 1, target_ref[1:2, :], tile)
        columns = jnp.transpose(tile)
        txy_ref[0] = jnp.broadcast_to(columns[:, 0:1], (rows, LANES))
        txy_ref[1] = jnp.broadcast_to(columns[:, 1:2], (rows, LANES))

    table = table_ref[...]
    bodies = table.shape[1]
    one_hot = (
        lax.broadcasted_iota(jnp.int32, (bodies, body_ref.shape[1]), 0) == body_ref[...]
    ).astype(jnp.bfloat16)
    high_part = table.astype(jnp.bfloat16)
    rest_one = table - high_part.astype(jnp.float32)
    middle_part = rest_one.astype(jnp.bfloat16)
    low_part = (rest_one - middle_part.astype(jnp.float32)).astype(jnp.bfloat16)
    picked = jnp.dot(high_part, one_hot, preferred_element_type=jnp.float32)
    picked = picked + jnp.dot(middle_part, one_hot, preferred_element_type=jnp.float32)
    coef_ref[...] = picked + jnp.dot(low_part, one_hot, preferred_element_type=jnp.float32)

    def one_sub(index, carry):
        row_at = pl.multiple_of((index // groups) * SUB_ROWS, SUB_ROWS)
        col_at = pl.multiple_of((index % groups) * LANES, LANES)
        tx = txy_ref[0, pl.ds(row_at, SUB_ROWS), :]
        ty = txy_ref[1, pl.ds(row_at, SUB_ROWS), :]
        sx = sxy_ref[pl.ds(0, 1), pl.ds(col_at, LANES)]
        sy = sxy_ref[pl.ds(1, 1), pl.ds(col_at, LANES)]
        delta_x = tx - sx
        delta_y = ty - sy
        radius = jnp.sqrt(delta_x * delta_x + delta_y * delta_y + 0.25)
        decay_rate = jnp.exp(-0.005 * radius)
        cos_part, sin_part = cos_and_sin(1.5 * radius)
        step_re = decay_rate * cos_part
        step_im = decay_rate * sin_part

        def coef(n):
            return (coef_ref[pl.ds(n, 1), pl.ds(col_at, LANES)],
                    coef_ref[pl.ds(terms + n, 1), pl.ds(col_at, LANES)])

        last_re, last_im = coef(terms - 1)
        total_re = jnp.broadcast_to(last_re, radius.shape)
        total_im = jnp.broadcast_to(last_im, radius.shape)
        for degree in range(terms - 2, -1, -1):
            c_re, c_im = coef(degree)
            next_re = total_re * step_re - total_im * step_im + c_re
            next_im = total_re * step_im + total_im * step_re + c_im
            total_re, total_im = next_re, next_im
        series_re = total_re * step_re - total_im * step_im
        series_im = total_re * step_im + total_im * step_re
        re_scr[pl.ds(row_at, SUB_ROWS), pl.ds(col_at, LANES)] = (1.0 / radius + series_re).astype(jnp.bfloat16)
        im_scr[pl.ds(row_at, SUB_ROWS), pl.ds(col_at, LANES)] = series_im.astype(jnp.bfloat16)
        return carry

    lax.fori_loop(0, (rows // SUB_ROWS) * groups, one_sub, 0, unroll=2)
    probe = probe_ref[...]
    rank = probe.shape[1]
    out_ref[:, :rank] += jnp.dot(re_scr[...], probe, preferred_element_type=jnp.float32)
    out_ref[:, rank:] += jnp.dot(im_scr[...], probe, preferred_element_type=jnp.float32)


def sketch_pallas(target_xy, source_xy, series_coef, body_of, probe_matrix):
    rows = target_xy.shape[1]
    sources = source_xy.shape[1]
    rank = probe_matrix.shape[1]
    col_block = min(COL_BLOCK, sources)
    table = series_coef.reshape(-1, series_coef.shape[2])
    return pl.pallas_call(
        sketch_kernel,
        grid=(sources // col_block,),
        in_specs=[
            pl.BlockSpec((2, rows), lambda j: (0, 0)),
            pl.BlockSpec((2, col_block), lambda j: (0, j)),
            pl.BlockSpec(table.shape, lambda j: (0, 0)),
            pl.BlockSpec((1, col_block), lambda j: (0, j)),
            pl.BlockSpec((col_block, rank), lambda j: (j, 0)),
        ],
        out_specs=pl.BlockSpec((rows, 2 * rank), lambda j: (0, 0)),
        out_shape=jax.ShapeDtypeStruct((rows, 2 * rank), jnp.float32),
        scratch_shapes=[pltpu.VMEM((2, rows, LANES), jnp.float32),
                        pltpu.VMEM((table.shape[0], col_block), jnp.float32),
                        pltpu.VMEM((rows, col_block), jnp.bfloat16),
                        pltpu.VMEM((rows, col_block), jnp.bfloat16)],
    )(target_xy, source_xy, table, body_of.reshape(1, sources), probe_matrix)


def factor_kernel(gram_ref, rows_ref, upper_ref, basis_ref, inverse_ref):
    size = gram_ref.shape[0]
    upper_ref[...] = gram_ref[...]
    rows = lax.broadcasted_iota(jnp.int32, (size, size), 0)
    cols = lax.broadcasted_iota(jnp.int32, (size, size), 1)
    inverse_ref[...] = jnp.where(rows == cols, 1.0, 0.0).astype(jnp.float32)
    lane = lax.broadcasted_iota(jnp.int32, (1, size), 1)
    sublane = lax.broadcasted_iota(jnp.int32, (size, 1), 0)

    def step(j, carry):
        left = upper_ref[...]
        row_left = upper_ref[pl.ds(j, 1), :]
        row_right = inverse_ref[pl.ds(j, 1), :]
        pivot = jnp.sum(jnp.where(lane == j, row_left, 0.0), axis=1, keepdims=True)
        scale = 1.0 / jnp.sqrt(pivot)
        pivot_left = jnp.where(lane >= j, row_left * scale, 0.0)
        pivot_right = row_right * scale
        column = jnp.sum(jnp.where(cols == j, left, 0.0), axis=1, keepdims=True)
        multiplier = jnp.where(sublane > j, column * scale, 0.0)
        upper_ref[...] = left - multiplier * pivot_left
        inverse_ref[...] = inverse_ref[...] - multiplier * pivot_right
        upper_ref[pl.ds(j, 1), :] = pivot_left
        inverse_ref[pl.ds(j, 1), :] = pivot_right
        return carry

    lax.fori_loop(0, size, step, 0)
    upper_ref[...] = jnp.where(rows <= cols, upper_ref[...], 0.0)
    inverse = inverse_ref[...]
    for half in range(rows_ref.shape[1] // size):
        basis_ref[:, half * size : (half + 1) * size] = lax.dot_general(
            rows_ref[:, half * size : (half + 1) * size],
            inverse,
            (((1,), (1,)), ((), ())),
            precision=lax.Precision.HIGHEST,
            preferred_element_type=jnp.float32,
        )


def factor_pallas(gram, own_rows):
    size = gram.shape[0]
    return pl.pallas_call(
        factor_kernel,
        out_shape=(jax.ShapeDtypeStruct((size, size), jnp.float32),
                   jax.ShapeDtypeStruct(own_rows.shape, jnp.float32)),
        scratch_shapes=[pltpu.VMEM((size, size), jnp.float32)],
    )(gram, own_rows)


def in_blocks(array, dim, count):
    shape = array.shape
    tiles = array.reshape(*shape[:dim], count, shape[dim] // count, *shape[dim + 1 :])
    return jnp.moveaxis(tiles, dim, 0)


def sent_and_summed(array, axis, dim):
    tiles = in_blocks(array, dim, lax.axis_size(axis))
    arrived = lax.all_to_all(tiles, axis, split_axis=0, concat_axis=0, tiled=True)
    return arrived.sum(axis=0)


def from_everyone(array, axis):
    copies = jnp.broadcast_to(array, (lax.axis_size(axis), *array.shape))
    return lax.all_to_all(copies, axis, split_axis=0, concat_axis=0, tiled=True)


def of_everyone(array, axis):
    everything = from_everyone(array, axis)
    return jnp.sum(everything, axis=0)


def panel_series(rows_xy, cols_xy, coef_re, coef_im):
    delta_x = rows_xy[0][:, None] - cols_xy[0][None, :]
    delta_y = rows_xy[1][:, None] - cols_xy[1][None, :]
    radius = jnp.sqrt(delta_x * delta_x + delta_y * delta_y + 0.25)
    decay_rate = jnp.exp(-0.005 * radius)
    step_re = decay_rate * jnp.cos(1.5 * radius)
    step_im = decay_rate * jnp.sin(1.5 * radius)
    term_count = coef_re.shape[0]
    total_re = jnp.broadcast_to(coef_re[term_count - 1][None, :], radius.shape)
    total_im = jnp.broadcast_to(coef_im[term_count - 1][None, :], radius.shape)
    for degree in range(term_count - 2, -1, -1):
        next_re = total_re * step_re - total_im * step_im + coef_re[degree][None, :]
        next_im = total_re * step_im + total_im * step_re + coef_im[degree][None, :]
        total_re, total_im = (next_re, next_im)
    series_re = total_re * step_re - total_im * step_im
    series_im = total_re * step_im + total_im * step_re
    tile_re = (1.0 / radius + series_re).astype(jnp.bfloat16)
    tile_im = series_im.astype(jnp.bfloat16)
    return (tile_re, tile_im)


def sketch_rows(target_xy, source_xy, picked, probe_matrix, row_count):
    source_count = probe_matrix.shape[0]
    block_width = math.gcd(source_count, 1024)
    blocks = source_count // block_width
    rank_width = probe_matrix.shape[1]

    def add_block(block_index, totals):
        block_start = block_index * block_width
        xy_block = lax.dynamic_slice_in_dim(source_xy, block_start, block_width, 1)
        coef_block = lax.dynamic_slice_in_dim(picked, block_start, block_width, 1)
        probe_block = lax.dynamic_slice_in_dim(probe_matrix, block_start, block_width, 0)
        tile_re, tile_im = panel_series(
            target_xy, xy_block, coef_block[:NTERMS], coef_block[NTERMS:]
        )
        part_re = jnp.dot(tile_re, probe_block, preferred_element_type=jnp.float32)
        part_im = jnp.dot(tile_im, probe_block, preferred_element_type=jnp.float32)
        return totals + jnp.concatenate([part_re, part_im], axis=1)

    start_totals = jnp.zeros((row_count, 2 * rank_width), jnp.float32)
    return lax.fori_loop(0, blocks, add_block, start_totals)


def gram_of(rows_part, scale_rows):
    rank_width = rows_part.shape[1] // 2
    stacked = rows_part.reshape(-1, rank_width)
    return jnp.dot(stacked.T, stacked, precision=lax.Precision.HIGHEST) / scale_rows


def pick_coefficients(series_coef, body_of):
    bodies = series_coef.shape[2]
    one_hot = (jnp.arange(bodies, dtype=jnp.int32)[:, None] == body_of[None, :]).astype(
        jnp.bfloat16
    )
    table = series_coef.reshape(-1, bodies)
    high_part = table.astype(jnp.bfloat16)
    rest_one = table - high_part.astype(jnp.float32)
    middle_part = rest_one.astype(jnp.bfloat16)
    low_part = (rest_one - middle_part.astype(jnp.float32)).astype(jnp.bfloat16)
    picked = jnp.dot(high_part, one_hot, preferred_element_type=jnp.float32)
    picked = picked + jnp.dot(middle_part, one_hot, preferred_element_type=jnp.float32)
    return picked + jnp.dot(low_part, one_hot, preferred_element_type=jnp.float32)


def per_device(target_xy, source_xy, body_of, series_coef, probe_matrix, row_weight):
    rank_width = probe_matrix.shape[1]
    rows_all = target_xy.shape[1]
    own_count = rows_all // lax.axis_size("src")
    scale_rows = float(2 * rows_all * lax.axis_size("tgt"))
    own_start = lax.axis_index("src") * own_count
    own_sum = sent_and_summed(
        sketch_pallas(target_xy, source_xy, series_coef, body_of, probe_matrix),
        "src",
        0,
    )
    own_weight = lax.dynamic_slice_in_dim(row_weight, own_start, own_count, 0)
    own_rows = own_sum * own_weight[:, None]
    local_gram = gram_of(own_rows, scale_rows)
    gram_piece = sent_and_summed(local_gram, "src", 0)
    gram_piece = of_everyone(gram_piece, "tgt")
    full_gram = from_everyone(gram_piece, "src").reshape(rank_width, rank_width)
    upper_factor, basis_rows = factor_pallas(full_gram, own_rows)
    return (basis_rows, upper_factor)


def solution(mesh):
    return jax.shard_map(
        per_device,
        mesh=mesh,
        in_specs=(P(None, "tgt"), P(None, "src"), P("src"), P(), P("src", None), P("tgt")),
        out_specs=(P(("tgt", "src"), None), P()),
        check_vma=False,
    )
```
